32 devices in a mesh: section: 2 (over core), dp: 16 (over z, y, x).
Axes of the slice: x: 2, y: 2, z: 4, core: 2. Of those that a mesh axis runs over, the one named last changes fastest.
Arguments:
- acts: bfloat16 [2, 16, 1, 64, 2, 2, 128], P('section', 'dp'), may hold values from -6 to 6
- preacts: bfloat16 [2, 16, 1, 64, 2, 2, 128], P('section', 'dp'), may hold values from -6 to 6
- top_grad: bfloat16 [16, 1, 64, 2, 2, 128], P('dp'), may hold values from -6 to 6
- weights: bfloat16 [2, 64, 1728], P('section'), may hold values from -0.21875 to 0.21875
- a_factor: bfloat16 [2, 1728, 1728], P('section', 'dp'), as said below
- g_factor: bfloat16 [2, 64, 64], P('section'), as said below
Outputs:
- act_grads: bfloat16 [2, 16, 1, 64, 2, 2, 128], P('section', 'dp')
- update: float32 [2, 1728, 64], P('section', 'dp')
- inverse: float32 [2, 1728, 1728], P('section', 'dp')
The draws below stay inside these ranges and needn't reach their ends.
Inputs may be any that keep to these rules, and one draw needn't show every extreme that they name: `a_factor`: each matrix is symmetric and positive definite. `g_factor`: each matrix is symmetric and positive definite.
All inputs are finite; a program needn't handle non-finite values. Where the reference program divides by a largest or mean magnitude, that divisor is 1e-20 or more.
Results may differ from the reference program's by a relative error of at most 0.006.
Values may be sent and summed in bfloat16 or wider, within the bound.
No kernel may reach another device: no remote copies, remote signals or barrier semaphores. Data moves between devices by JAX's collectives and lax.ppermute only.
A program may use at most 64 MiB of HBM per device.

```python
import math
import jax
import jax.numpy as jnp
from jax import lax

C = 64
KW = 3
VX = 2
VY = 2
VZ = 128
MICRO = 1
TAPS = 27
OA = 1728
SECTIONS = 2
REPLICAS = 16
N_SECTION = 2
N_DP = 16


def spd_matrices(key, count, order_full):
    key_perm, key_noise, key_scale = jax.random.split(key, 3)
    decay = 0.9
    orders = jax.vmap(lambda one_key: jax.random.permutation(one_key, order_full))(jax.random.split(key_perm, count))
    distance = jnp.abs(orders[:, :, None] - orders[:, None, :]).astype(jnp.float32)
    kernel = jnp.exp(distance * math.log(decay))
    integers = jax.random.randint(key_noise, (count, order_full, order_full), -2, 3).astype(jnp.float32)
    wishart = jnp.einsum('cik,cjk->cij', integers, integers, precision=lax.Precision.HIGHEST) / (2.0 * order_full)
    identity = jnp.eye(order_full, dtype=jnp.float32)
    base_matrix = kernel + 0.1 * wishart + 0.05 * identity[None]
    ramp_up = 1.0 + 2.0 * jnp.arange(order_full, dtype=jnp.float32) / max(order_full - 1, 1)
    spread = jax.random.uniform(key_scale, (count, order_full), jnp.float32, 0.5, 1.5)
    scales = ramp_up[None, :] * spread
    root_scale = jnp.sqrt(scales)
    return base_matrix * root_scale[:, :, None] * root_scale[:, None, :]


def draw_a_factor(key, part):
    return spd_matrices(jax.random.fold_in(key, 11), SECTIONS, OA).astype(jnp.bfloat16)


def draw_g_factor(key, part):
    return spd_matrices(jax.random.fold_in(key, 23), SECTIONS, C).astype(jnp.bfloat16)


def shard_levels(own_key, dims, shards, smallest, top_value):
    def one(position, shards_of):
        draws = jax.random.uniform(jax.random.fold_in(jax.random.fold_in(own_key, 6), position), (shards_of,), jnp.float32, smallest / len(shards), top_value / len(shards))
        return jnp.repeat(jnp.exp(draws), dims[position] // shards_of).reshape((-1,) + (1,) * (len(dims) - position - 1))

    factor_of = one(*shards[0])
    for cut in shards[1:]:
        factor_of = factor_of * one(*cut)
    return factor_of


def scatter_about(key, dims, scale, bound, cuts=(), kind=jnp.bfloat16):
    entries = scale * jax.random.normal(key, dims, jnp.float32)
    if cuts:
        entries = entries * shard_levels(key, dims, cuts, -0.22, 0.18)
    return jnp.clip(entries, -bound, bound).astype(kind)


def setup_inputs(seed: int = 0) -> dict:
    key_of = jax.random.split(jax.random.key(seed), 7)
    return {
        "acts": scatter_about(key_of[0], (SECTIONS, REPLICAS, MICRO, C, VX, VY, VZ), 1.0, 6.0, ((0, 2), (1, 16))),
        "preacts": scatter_about(key_of[1], (SECTIONS, REPLICAS, MICRO, C, VX, VY, VZ), 1.0, 6.0, ((0, 2), (1, 16))),
        "top_grad": scatter_about(key_of[2], (REPLICAS, MICRO, C, VX, VY, VZ), 1.0, 6.0, ((0, 16),)),
        "weights": scatter_about(key_of[3], (SECTIONS, C, OA), (TAPS * C // 2) ** -0.5, 0.21875, ((0, 2),)),
        "a_factor": draw_a_factor(jax.random.fold_in(key_of[6], 71), 0),
        "g_factor": draw_g_factor(jax.random.fold_in(key_of[6], 71), 0),
    }


def tap_offsets(kernel_width):
    middle = kernel_width // 2
    result = []
    for along_x in range(kernel_width):
        for along_y in range(kernel_width):
            for along_z in range(kernel_width):
                result.append((along_x - middle, along_y - middle, along_z - middle))
    return result


def taps_stack(volume, kernel_width, direction):
    middle = kernel_width // 2
    padded = jnp.pad(volume, ((0, 0), (middle, middle), (middle, middle), (middle, middle)))
    size_x, size_y, size_z = volume.shape[1], volume.shape[2], volume.shape[3]
    pieces = []
    for off_x, off_y, off_z in tap_offsets(kernel_width):
        start_x = middle + direction * off_x
        start_y = middle + direction * off_y
        start_z = middle + direction * off_z
        pieces.append(padded[:, start_x:start_x + size_x, start_y:start_y + size_y, start_z:start_z + size_z])
    stacked = jnp.stack(pieces, 0)
    return stacked.reshape(len(pieces) * volume.shape[0], size_x * size_y * size_z)


def back_input(grad_out, w_rows):
    columns = taps_stack(grad_out, KW, -1)
    summed = lax.dot_general(w_rows.astype(jnp.float32), columns.astype(jnp.float32), (((0,), (0,)), ((), ())))
    return summed.astype(jnp.bfloat16).reshape(grad_out.shape)


def back_weight(volume, grad_out):
    columns = taps_stack(volume, KW, 1)
    flattened = grad_out.reshape(grad_out.shape[0], -1)
    return lax.dot_general(columns.astype(jnp.float32), flattened.astype(jnp.float32), (((1,), (1,)), ((), ())))


def newton_inverse(matrix):
    values = matrix.astype(jnp.float32)
    step_size = 1.0 / jnp.max(jnp.sum(jnp.abs(values), axis=1))
    identity = jnp.eye(matrix.shape[0], dtype=jnp.float32)
    resid0 = (identity - step_size * values).astype(jnp.bfloat16)
    resid1 = jnp.dot(resid0.astype(jnp.float32), resid0.astype(jnp.float32)).astype(jnp.bfloat16)
    cross_term = jnp.dot(resid1.astype(jnp.float32), resid0.astype(jnp.float32))
    return step_size * (identity + resid0.astype(jnp.float32) + resid1.astype(jnp.float32) + cross_term)


def reference(acts, preacts, top_grad, weights, a_factor, g_factor):
    section_grads = [None] * N_SECTION
    updates = [None] * N_SECTION
    inverses = [None] * N_SECTION
    for section_now in reversed(range(N_SECTION)):
        w_rows = weights[section_now].reshape(C, TAPS, C).transpose(1, 0, 2).reshape(TAPS * C, C)
        if section_now == N_SECTION - 1:
            arriving_all = top_grad
        else:
            arriving_all = section_grads[section_now + 1]

        def replica_pass(operands):
            inputs, pre_values, arriving = operands
            sent = []
            grad_sum = jnp.zeros((OA, C), jnp.float32)
            for micro in range(MICRO):
                grad_out = jnp.where(pre_values[micro] > 0, arriving[micro], jnp.zeros_like(arriving[micro]))
                sent.append(back_input(grad_out, w_rows))
                grad_sum = grad_sum + back_weight(inputs[micro], grad_out)
            return jnp.stack(sent, 0), grad_sum

        sent_all, local_grads = lax.map(replica_pass, (acts[section_now], preacts[section_now], arriving_all))
        section_grads[section_now] = sent_all
        mean_grad = jnp.sum(local_grads, axis=0) / N_DP
        inverse_now = newton_inverse(a_factor[section_now])
        g_inverse = newton_inverse(g_factor[section_now])
        preconditioned = jnp.dot(mean_grad, g_inverse, precision=lax.Precision.HIGHEST, preferred_element_type=jnp.float32)
        updates[section_now] = jnp.dot(inverse_now, preconditioned, precision=lax.Precision.HIGHEST, preferred_element_type=jnp.float32)
        inverses[section_now] = inverse_now
    return jnp.stack(section_grads, 0), jnp.stack(updates, 0), jnp.stack(inverses, 0)
```

```python
import jax
import jax.numpy as jnp
from jax import lax
from jax.sharding import PartitionSpec as P

KW = 3
MICRO = 1


def shifted(value, axis, steps):
    count = lax.axis_size(axis)
    first, last = (max(0, -steps), min(count, count - steps))
    return lax.ppermute(value, axis, [(source, source + steps) for source in range(first, last)])


def tap_offsets(kernel_width):
    middle = kernel_width // 2
    result = []
    for along_x in range(kernel_width):
        for along_y in range(kernel_width):
            for along_z in range(kernel_width):
                result.append((along_x - middle, along_y - middle, along_z - middle))
    return result


def taps_stack(volume, kernel_width, direction):
    middle = kernel_width // 2
    padded = jnp.pad(volume, ((0, 0), (middle, middle), (middle, middle), (middle, middle)))
    size_x, size_y, size_z = (volume.shape[1], volume.shape[2], volume.shape[3])
    pieces = []
    for off_x, off_y, off_z in tap_offsets(kernel_width):
        start_x = middle + direction * off_x
        start_y = middle + direction * off_y
        start_z = middle + direction * off_z
        pieces.append(
            padded[
                :,
                start_x : start_x + size_x,
                start_y : start_y + size_y,
                start_z : start_z + size_z,
            ]
        )
    stacked = jnp.stack(pieces, 0)
    return stacked.reshape(len(pieces) * volume.shape[0], size_x * size_y * size_z)


def back_input(grad_out, w_rows):
    columns = taps_stack(grad_out, KW, -1)
    summed = lax.dot_general(
        w_rows, columns, (((0,), (0,)), ((), ())), preferred_element_type=jnp.float32
    )
    return summed.astype(jnp.bfloat16).reshape(grad_out.shape)


def back_weight(volume, grad_out):
    columns = taps_stack(volume, KW, 1)
    flattened = grad_out.reshape(grad_out.shape[0], -1)
    return lax.dot_general(
        columns, flattened, (((1,), (1,)), ((), ())), preferred_element_type=jnp.float32
    )


def local_inverse(matrix):
    values = matrix.astype(jnp.float32)
    step_size = 1.0 / jnp.max(jnp.sum(jnp.abs(values), axis=1))
    identity = jnp.eye(matrix.shape[0], dtype=jnp.float32)
    resid0 = (identity - step_size * values).astype(jnp.bfloat16)
    resid1 = jnp.dot(resid0, resid0, preferred_element_type=jnp.float32).astype(jnp.bfloat16)
    cross_term = jnp.dot(resid1, resid0, preferred_element_type=jnp.float32)
    return step_size * (
        identity + resid0.astype(jnp.float32) + resid1.astype(jnp.float32) + cross_term
    )


def eye_rows(start_row, row_total, order_full):
    column_ids = lax.broadcasted_iota(jnp.int32, (row_total, order_full), 1)
    row_ids = lax.broadcasted_iota(jnp.int32, (row_total, order_full), 0)
    return (column_ids == start_row + row_ids).astype(jnp.float32)


def doubling_sum(value, axis):
    count = lax.axis_size(axis)
    assert count & (count - 1) == 0
    stride = 1
    while stride < count:
        value = value + lax.ppermute(value, axis, [(i, i ^ stride) for i in range(count)])
        stride *= 2
    return value


def shards(acts, preacts, top_grad, weights, a_factor, g_factor):
    section_index = lax.axis_index("section")
    section_count = lax.axis_size("section")
    tick_count = MICRO + section_count - 1
    gathered = lax.all_gather(a_factor[0], "dp", axis=0, tiled=True)
    inputs = acts[0, 0]
    pre_values = preacts[0, 0]
    upper_grads = top_grad[0]
    channels = weights.shape[1]
    w_rows = weights[0].reshape(channels, -1, channels).transpose(1, 0, 2).reshape(-1, channels)
    zero_field = jnp.zeros(inputs.shape[1:], jnp.bfloat16)

    def one_tick(tick_index, carried):
        outgoing, stored_grads, stored_slopes = carried
        incoming = shifted(outgoing, "section", -1)
        micro_index = tick_index - (section_count - 1 - section_index)
        is_valid = jnp.logical_and(micro_index >= 0, micro_index < MICRO)
        clipped = jnp.clip(micro_index, 0, MICRO - 1)
        from_top = lax.dynamic_index_in_dim(upper_grads, clipped, 0, keepdims=False)
        arriving = jnp.where(section_index == section_count - 1, from_top, incoming)
        pre_now = lax.dynamic_index_in_dim(pre_values, clipped, 0, keepdims=False)
        grad_out = jnp.where(pre_now > 0, arriving, zero_field)
        sending = back_input(grad_out, w_rows)
        old_grad = lax.dynamic_index_in_dim(stored_grads, clipped, 0, keepdims=False)
        old_slope = lax.dynamic_index_in_dim(stored_slopes, clipped, 0, keepdims=False)
        stored_grads = lax.dynamic_update_index_in_dim(
            stored_grads, jnp.where(is_valid, sending, old_grad), clipped, 0
        )
        stored_slopes = lax.dynamic_update_index_in_dim(
            stored_slopes, jnp.where(is_valid, grad_out, old_slope), clipped, 0
        )
        return (sending, stored_grads, stored_slopes)

    start_state = (
        zero_field,
        jnp.zeros(inputs.shape, jnp.bfloat16),
        jnp.zeros(inputs.shape, jnp.bfloat16),
    )
    last_sent, stored_grads, stored_slopes = lax.fori_loop(0, tick_count, one_tick, start_state)
    local_grad = back_weight(inputs[0], stored_slopes[0])
    summed_grad = doubling_sum(local_grad, "dp")
    mean_grad = summed_grad / lax.axis_size("dp")
    a_rows = a_factor[0]
    row_total = a_rows.shape[0]
    order_full = a_rows.shape[1]
    first_row = lax.axis_index("dp") * row_total
    full_values = gathered.astype(jnp.float32)
    step_size = 1.0 / jnp.max(jnp.sum(jnp.abs(full_values), axis=1))
    full_resid0 = (jnp.eye(order_full, dtype=jnp.float32) - step_size * full_values).astype(jnp.bfloat16)
    own_eye = eye_rows(first_row, row_total, order_full)
    resid0 = (own_eye - step_size * a_rows.astype(jnp.float32)).astype(jnp.bfloat16)
    resid1 = jnp.dot(resid0, full_resid0, preferred_element_type=jnp.float32).astype(jnp.bfloat16)
    cross_term = jnp.dot(resid1, full_resid0, preferred_element_type=jnp.float32)
    inverse_rows = step_size * (
        own_eye + resid0.astype(jnp.float32) + resid1.astype(jnp.float32) + cross_term
    )
    g_inverse = local_inverse(g_factor[0])
    preconditioned = jnp.dot(
        mean_grad, g_inverse, precision=lax.Precision.HIGHEST, preferred_element_type=jnp.float32
    )
    update_rows = jnp.dot(
        inverse_rows,
        preconditioned,
        precision=lax.Precision.HIGHEST,
        preferred_element_type=jnp.float32,
    )
    return (stored_grads[None, None], update_rows[None], inverse_rows[None])


def solution(mesh):
    placed = (
        P("section", "dp", None, None, None, None, None),
        P("section", "dp", None, None, None, None, None),
        P("dp", None, None, None, None, None),
        P("section", None, None),
        P("section", "dp", None),
        P("section", None, None),
    )
    return jax.shard_map(
        shards,
        mesh=mesh,
        in_specs=placed,
        out_specs=(
            P("section", "dp", None, None, None, None, None),
            P("section", "dp", None),
            P("section", "dp", None),
        ),
        check_vma=False,
    )
```

```python
import jax
import jax.numpy as jnp
from jax import lax
from jax.sharding import PartitionSpec as P

KW = 3
MICRO = 1


def shifted(value, axis, steps):
    count = lax.axis_size(axis)
    first, last = (max(0, -steps), min(count, count - steps))
    return lax.ppermute(value, axis, [(source, source + steps) for source in range(first, last)])


def tap_offsets(kernel_width):
    middle = kernel_width // 2
    result = []
    for along_x in range(kernel_width):
        for along_y in range(kernel_width):
            for along_z in range(kernel_width):
                result.append((along_x - middle, along_y - middle, along_z - middle))
    return result


def taps_stack(volume, kernel_width, direction):
    middle = kernel_width // 2
    padded = jnp.pad(volume, ((0, 0), (middle, middle), (middle, middle), (middle, middle)))
    size_x, size_y, size_z = (volume.shape[1], volume.shape[2], volume.shape[3])
    pieces = []
    for off_x, off_y, off_z in tap_offsets(kernel_width):
        start_x = middle + direction * off_x
        start_y = middle + direction * off_y
        start_z = middle + direction * off_z
        pieces.append(
            padded[
                :,
                start_x : start_x + size_x,
                start_y : start_y + size_y,
                start_z : start_z + size_z,
            ]
        )
    stacked = jnp.stack(pieces, 0)
    return stacked.reshape(len(pieces) * volume.shape[0], size_x * size_y * size_z)


def back_input(grad_out, w_rows):
    columns = taps_stack(grad_out, KW, -1)
    summed = lax.dot_general(
        w_rows, columns, (((0,), (0,)), ((), ())), preferred_element_type=jnp.float32
    )
    return summed.astype(jnp.bfloat16).reshape(grad_out.shape)


def back_weight(volume, grad_out):
    columns = taps_stack(volume, KW, 1)
    flattened = grad_out.reshape(grad_out.shape[0], -1)
    return lax.dot_general(
        columns, flattened, (((1,), (1,)), ((), ())), preferred_element_type=jnp.float32
    )


def local_inverse(matrix):
    values = matrix.astype(jnp.float32)
    step_size = 1.0 / jnp.max(jnp.sum(jnp.abs(values), axis=1))
    identity = jnp.eye(matrix.shape[0], dtype=jnp.float32)
    resid0 = (identity - step_size * values).astype(jnp.bfloat16)
    resid1 = jnp.dot(resid0, resid0, preferred_element_type=jnp.float32).astype(jnp.bfloat16)
    cross_term = jnp.dot(resid1, resid0, preferred_element_type=jnp.float32)
    return step_size * (
        identity + resid0.astype(jnp.float32) + resid1.astype(jnp.float32) + cross_term
    )


def eye_rows(start_row, row_total, order_full):
    column_ids = lax.broadcasted_iota(jnp.int32, (row_total, order_full), 1)
    row_ids = lax.broadcasted_iota(jnp.int32, (row_total, order_full), 0)
    return (column_ids == start_row + row_ids).astype(jnp.float32)


def halving_sum(value, axis):
    count = lax.axis_size(axis)
    assert count & (count - 1) == 0 and value.shape[0] % count == 0
    index = lax.axis_index(axis)
    stride = count // 2
    while stride >= 1:
        half = value.shape[0] // 2
        upper = (index // stride) % 2 == 1
        keep = jnp.where(upper, value[half:], value[:half])
        send = jnp.where(upper, value[:half], value[half:])
        value = keep + lax.ppermute(send, axis, [(i, i ^ stride) for i in range(count)])
        stride //= 2
    stride = 1
    while stride < count:
        other = lax.ppermute(value, axis, [(i, i ^ stride) for i in range(count)])
        upper = (index // stride) % 2 == 1
        value = jnp.where(upper, jnp.concatenate([other, value]), jnp.concatenate([value, other]))
        stride *= 2
    return value


def shards(acts, preacts, top_grad, weights, a_factor, g_factor):
    section_index = lax.axis_index("section")
    section_count = lax.axis_size("section")
    tick_count = MICRO + section_count - 1
    gathered = lax.all_gather(a_factor[0], "dp", axis=0)
    inputs = acts[0, 0]
    pre_values = preacts[0, 0]
    upper_grads = top_grad[0]
    channels = weights.shape[1]
    w_rows = weights[0].reshape(channels, -1, channels).transpose(1, 0, 2).reshape(-1, channels)
    zero_field = jnp.zeros(inputs.shape[1:], jnp.bfloat16)

    def one_tick(tick_index, carried):
        outgoing, stored_grads, stored_slopes = carried
        incoming = shifted(outgoing, "section", -1)
        micro_index = tick_index - (section_count - 1 - section_index)
        is_valid = jnp.logical_and(micro_index >= 0, micro_index < MICRO)
        clipped = jnp.clip(micro_index, 0, MICRO - 1)
        from_top = lax.dynamic_index_in_dim(upper_grads, clipped, 0, keepdims=False)
        arriving = jnp.where(section_index == section_count - 1, from_top, incoming)
        pre_now = lax.dynamic_index_in_dim(pre_values, clipped, 0, keepdims=False)
        grad_out = jnp.where(pre_now > 0, arriving, zero_field)
        sending = back_input(grad_out, w_rows)
        old_grad = lax.dynamic_index_in_dim(stored_grads, clipped, 0, keepdims=False)
        old_slope = lax.dynamic_index_in_dim(stored_slopes, clipped, 0, keepdims=False)
        stored_grads = lax.dynamic_update_index_in_dim(
            stored_grads, jnp.where(is_valid, sending, old_grad), clipped, 0
        )
        stored_slopes = lax.dynamic_update_index_in_dim(
            stored_slopes, jnp.where(is_valid, grad_out, old_slope), clipped, 0
        )
        return (sending, stored_grads, stored_slopes)

    start_state = (
        zero_field,
        jnp.zeros(inputs.shape, jnp.bfloat16),
        jnp.zeros(inputs.shape, jnp.bfloat16),
    )
    last_sent, stored_grads, stored_slopes = lax.fori_loop(0, tick_count, one_tick, start_state)
    local_grad = back_weight(inputs[0], stored_slopes[0])
    summed_grad = halving_sum(local_grad, "dp")
    mean_grad = summed_grad / lax.axis_size("dp")
    a_rows = a_factor[0]
    row_total = a_rows.shape[0]
    order_full = a_rows.shape[1]
    first_row = lax.axis_index("dp") * row_total
    full_values = gathered.astype(jnp.float32)
    step_size = 1.0 / jnp.max(jnp.sum(jnp.abs(full_values), axis=2))
    shard_count = gathered.shape[0]
    block_ids = lax.broadcasted_iota(jnp.int32, gathered.shape, 0)
    row_ids = lax.broadcasted_iota(jnp.int32, gathered.shape, 1)
    column_ids = lax.broadcasted_iota(jnp.int32, gathered.shape, 2)
    full_eye = (column_ids == block_ids * row_total + row_ids).astype(jnp.float32)
    full_resid0 = (full_eye - step_size * full_values).astype(jnp.bfloat16)
    contract = (((1, 2), (0, 1)), ((), ()))
    own_eye = eye_rows(first_row, row_total, order_full)
    resid0 = (own_eye - step_size * a_rows.astype(jnp.float32)).astype(jnp.bfloat16)
    resid1 = lax.dot_general(
        resid0.reshape(row_total, shard_count, row_total), full_resid0, contract,
        preferred_element_type=jnp.float32,
    ).astype(jnp.bfloat16)
    cross_term = lax.dot_general(
        resid1.reshape(row_total, shard_count, row_total), full_resid0, contract,
        preferred_element_type=jnp.float32,
    )
    inverse_rows = step_size * (
        own_eye + resid0.astype(jnp.float32) + resid1.astype(jnp.float32) + cross_term
    )
    g_inverse = local_inverse(g_factor[0])
    preconditioned = jnp.dot(
        mean_grad, g_inverse, precision=lax.Precision.HIGHEST, preferred_element_type=jnp.float32
    )
    update_rows = jnp.dot(
        inverse_rows,
        preconditioned,
        precision=lax.Precision.HIGHEST,
        preferred_element_type=jnp.float32,
    )
    return (stored_grads[None, None], update_rows[None], inverse_rows[None])


def solution(mesh):
    placed = (
        P("section", "dp", None, None, None, None, None),
        P("section", "dp", None, None, None, None, None),
        P("dp", None, None, None, None, None),
        P("section", None, None),
        P("section", "dp", None),
        P("section", None, None),
    )
    return jax.shard_map(
        shards,
        mesh=mesh,
        in_specs=placed,
        out_specs=(
            P("section", "dp", None, None, None, None, None),
            P("section", "dp", None),
            P("section", "dp", None),
        ),
        check_vma=False,
    )
```

```python
import jax
import jax.numpy as jnp
from jax import lax
from jax.sharding import PartitionSpec as P

KW = 3
MICRO = 1


def shifted(value, axis, steps):
    count = lax.axis_size(axis)
    first, last = (max(0, -steps), min(count, count - steps))
    return lax.ppermute(value, axis, [(source, source + steps) for source in range(first, last)])


def tap_offsets(kernel_width):
    middle = kernel_width // 2
    result = []
    for along_x in range(kernel_width):
        for along_y in range(kernel_width):
            for along_z in range(kernel_width):
                result.append((along_x - middle, along_y - middle, along_z - middle))
    return result


def taps_stack(volume, kernel_width, direction):
    middle = kernel_width // 2
    padded = jnp.pad(volume, ((0, 0), (middle, middle), (middle, middle), (middle, middle)))
    size_x, size_y, size_z = (volume.shape[1], volume.shape[2], volume.shape[3])
    pieces = []
    for off_x, off_y, off_z in tap_offsets(kernel_width):
        start_x = middle + direction * off_x
        start_y = middle + direction * off_y
        start_z = middle + direction * off_z
        pieces.append(
            padded[
                :,
                start_x : start_x + size_x,
                start_y : start_y + size_y,
                start_z : start_z + size_z,
            ]
        )
    stacked = jnp.stack(pieces, 0)
    return stacked.reshape(len(pieces) * volume.shape[0], size_x * size_y * size_z)


def back_input(grad_out, w_rows):
    columns = taps_stack(grad_out, KW, -1)
    summed = lax.dot_general(
        w_rows, columns, (((0,), (0,)), ((), ())), preferred_element_type=jnp.float32
    )
    return summed.astype(jnp.bfloat16).reshape(grad_out.shape)


def back_weight(volume, grad_out):
    columns = taps_stack(volume, KW, 1)
    flattened = grad_out.reshape(grad_out.shape[0], -1)
    return lax.dot_general(
        columns, flattened, (((1,), (1,)), ((), ())), preferred_element_type=jnp.float32
    )


def local_inverse(matrix):
    values = matrix.astype(jnp.float32)
    step_size = 1.0 / jnp.max(jnp.sum(jnp.abs(values), axis=1))
    identity = jnp.eye(matrix.shape[0], dtype=jnp.float32)
    resid0 = (identity - step_size * values).astype(jnp.bfloat16)
    resid1 = jnp.dot(resid0, resid0, preferred_element_type=jnp.float32).astype(jnp.bfloat16)
    cross_term = jnp.dot(resid1, resid0, preferred_element_type=jnp.float32)
    return step_size * (
        identity + resid0.astype(jnp.float32) + resid1.astype(jnp.float32) + cross_term
    )


def eye_rows(start_row, row_total, order_full):
    column_ids = lax.broadcasted_iota(jnp.int32, (row_total, order_full), 1)
    row_ids = lax.broadcasted_iota(jnp.int32, (row_total, order_full), 0)
    return (column_ids == start_row + row_ids).astype(jnp.float32)


def halving_sum(value, axis):
    count = lax.axis_size(axis)
    assert count & (count - 1) == 0 and value.shape[0] % count == 0
    index = lax.axis_index(axis)
    stride = 1
    while stride < count:
        half = value.shape[0] // 2
        upper = (index // stride) % 2 == 1
        keep = jnp.where(upper, value[half:], value[:half])
        send = jnp.where(upper, value[:half], value[half:])
        value = keep + lax.ppermute(send, axis, [(i, i ^ stride) for i in range(count)])
        stride *= 2
    stride = count // 2
    while stride >= 1:
        other = lax.ppermute(value, axis, [(i, i ^ stride) for i in range(count)])
        upper = (index // stride) % 2 == 1
        value = jnp.where(upper, jnp.concatenate([other, value]), jnp.concatenate([value, other]))
        stride //= 2
    return value


def compressed_products(gathered, a_rows, own_eye, shard_count, row_total):
    kept = shard_count // 2 + 1
    order_full = a_rows.shape[1]
    mirrored = shard_count - kept
    magnitudes = jnp.abs(gathered.astype(jnp.float32))
    direct_sums = jnp.sum(jnp.sum(magnitudes, axis=3), axis=1)
    column_sums = jnp.sum(magnitudes, axis=2)
    for offset in range(1, mirrored + 1):
        direct_sums = direct_sums + jnp.roll(column_sums[:, offset], offset, axis=0)
    step_size = 1.0 / jnp.max(direct_sums)
    block_eye = jnp.logical_and(
        lax.broadcasted_iota(jnp.int32, gathered.shape, 1) == 0,
        lax.broadcasted_iota(jnp.int32, gathered.shape, 2)
        == lax.broadcasted_iota(jnp.int32, gathered.shape, 3),
    ).astype(jnp.float32)
    resid_blocks = (block_eye - step_size * gathered.astype(jnp.float32)).astype(jnp.bfloat16)
    direct_right = jnp.stack(
        [jnp.roll(resid_blocks[:, offset], offset, axis=0) for offset in range(kept)], 0
    )
    mirror_right = resid_blocks[:, 1 : mirrored + 1].transpose(1, 0, 2, 3)

    def times_resid0(left_rows):
        left = left_rows.reshape(row_total, shard_count, row_total).transpose(1, 0, 2)
        direct_left = jnp.stack([jnp.roll(left, offset, axis=0) for offset in range(kept)], 0)
        mirror_left = jnp.stack(
            [jnp.roll(left, -offset, axis=0) for offset in range(1, mirrored + 1)], 0
        )
        product = jnp.einsum(
            "kjab,kjbc->jac", direct_left, direct_right, preferred_element_type=jnp.float32
        ) + jnp.einsum(
            "mjab,mjcb->jac", mirror_left, mirror_right, preferred_element_type=jnp.float32
        )
        return product.transpose(1, 0, 2).reshape(row_total, order_full)

    resid0 = (own_eye - step_size * a_rows.astype(jnp.float32)).astype(jnp.bfloat16)
    resid1 = times_resid0(resid0).astype(jnp.bfloat16)
    cross_term = times_resid0(resid1)
    return step_size, resid0, resid1, cross_term


def dense_products(gathered, a_rows, own_eye):
    row_total = a_rows.shape[0]
    shard_count = gathered.shape[0]
    full_values = gathered.astype(jnp.float32)
    step_size = 1.0 / jnp.max(jnp.sum(jnp.abs(full_values), axis=2))
    block_ids = lax.broadcasted_iota(jnp.int32, gathered.shape, 0)
    row_ids = lax.broadcasted_iota(jnp.int32, gathered.shape, 1)
    column_ids = lax.broadcasted_iota(jnp.int32, gathered.shape, 2)
    full_eye = (column_ids == block_ids * row_total + row_ids).astype(jnp.float32)
    full_resid0 = (full_eye - step_size * full_values).astype(jnp.bfloat16)
    contract = (((1, 2), (0, 1)), ((), ()))
    resid0 = (own_eye - step_size * a_rows.astype(jnp.float32)).astype(jnp.bfloat16)
    resid1 = lax.dot_general(
        resid0.reshape(row_total, shard_count, row_total), full_resid0, contract,
        preferred_element_type=jnp.float32,
    ).astype(jnp.bfloat16)
    cross_term = lax.dot_general(
        resid1.reshape(row_total, shard_count, row_total), full_resid0, contract,
        preferred_element_type=jnp.float32,
    )
    return step_size, resid0, resid1, cross_term


def shards(acts, preacts, top_grad, weights, a_factor, g_factor):
    section_index = lax.axis_index("section")
    section_count = lax.axis_size("section")
    tick_count = MICRO + section_count - 1
    shard_count = lax.axis_size("dp")
    row_total = a_factor.shape[1]
    compressed = shard_count % 2 == 0 and row_total >= 64
    if compressed:
        kept = shard_count // 2 + 1
        own_blocks = a_factor[0].reshape(row_total, shard_count, row_total).transpose(1, 0, 2)
        twice = jnp.concatenate([own_blocks, own_blocks], axis=0)
        upper_blocks = lax.dynamic_slice_in_dim(twice, lax.axis_index("dp"), kept, 0)
        gathered = lax.all_gather(upper_blocks, "dp", axis=0)
    else:
        gathered = lax.all_gather(a_factor[0], "dp", axis=0)
    inputs = acts[0, 0]
    pre_values = preacts[0, 0]
    upper_grads = top_grad[0]
    channels = weights.shape[1]
    w_rows = weights[0].reshape(channels, -1, channels).transpose(1, 0, 2).reshape(-1, channels)
    zero_field = jnp.zeros(inputs.shape[1:], jnp.bfloat16)

    def one_tick(tick_index, carried):
        outgoing, stored_grads, stored_slopes = carried
        incoming = shifted(outgoing, "section", -1)
        micro_index = tick_index - (section_count - 1 - section_index)
        is_valid = jnp.logical_and(micro_index >= 0, micro_index < MICRO)
        clipped = jnp.clip(micro_index, 0, MICRO - 1)
        from_top = lax.dynamic_index_in_dim(upper_grads, clipped, 0, keepdims=False)
        arriving = jnp.where(section_index == section_count - 1, from_top, incoming)
        pre_now = lax.dynamic_index_in_dim(pre_values, clipped, 0, keepdims=False)
        grad_out = jnp.where(pre_now > 0, arriving, zero_field)
        sending = back_input(grad_out, w_rows)
        old_grad = lax.dynamic_index_in_dim(stored_grads, clipped, 0, keepdims=False)
        old_slope = lax.dynamic_index_in_dim(stored_slopes, clipped, 0, keepdims=False)
        stored_grads = lax.dynamic_update_index_in_dim(
            stored_grads, jnp.where(is_valid, sending, old_grad), clipped, 0
        )
        stored_slopes = lax.dynamic_update_index_in_dim(
            stored_slopes, jnp.where(is_valid, grad_out, old_slope), clipped, 0
        )
        return (sending, stored_grads, stored_slopes)

    start_state = (
        zero_field,
        jnp.zeros(inputs.shape, jnp.bfloat16),
        jnp.zeros(inputs.shape, jnp.bfloat16),
    )
    last_sent, stored_grads, stored_slopes = lax.fori_loop(0, tick_count, one_tick, start_state)
    local_grad = back_weight(inputs[0], stored_slopes[0])
    summed_grad = halving_sum(local_grad, "dp")
    mean_grad = summed_grad / lax.axis_size("dp")
    a_rows = a_factor[0]
    order_full = a_rows.shape[1]
    first_row = lax.axis_index("dp") * row_total
    own_eye = eye_rows(first_row, row_total, order_full)
    if compressed:
        step_size, resid0, resid1, cross_term = compressed_products(
            gathered, a_rows, own_eye, shard_count, row_total
        )
    else:
        step_size, resid0, resid1, cross_term = dense_products(gathered, a_rows, own_eye)
    inverse_rows = step_size * (
        own_eye + resid0.astype(jnp.float32) + resid1.astype(jnp.float32) + cross_term
    )
    g_inverse = local_inverse(g_factor[0])
    preconditioned = jnp.dot(
        mean_grad, g_inverse, precision=lax.Precision.HIGHEST, preferred_element_type=jnp.float32
    )
    update_rows = jnp.dot(
        inverse_rows,
        preconditioned,
        precision=lax.Precision.HIGHEST,
        preferred_element_type=jnp.float32,
    )
    return (stored_grads[None, None], update_rows[None], inverse_rows[None])


def solution(mesh):
    placed = (
        P("section", "dp", None, None, None, None, None),
        P("section", "dp", None, None, None, None, None),
        P("dp", None, None, None, None, None),
        P("section", None, None),
        P("section", "dp", None),
        P("section", None, None),
    )
    return jax.shard_map(
        shards,
        mesh=mesh,
        in_specs=placed,
        out_specs=(
            P("section", "dp", None, None, None, None, None),
            P("section", "dp", None),
            P("section", "dp", None),
        ),
        check_vma=False,
    )
```

```python
import jax
import jax.numpy as jnp
from jax import lax
from jax.sharding import PartitionSpec as P

KW = 3
MICRO = 1


def shifted(value, axis, steps):
    count = lax.axis_size(axis)
    first, last = (max(0, -steps), min(count, count - steps))
    return lax.ppermute(value, axis, [(source, source + steps) for source in range(first, last)])


def tap_offsets(kernel_width):
    middle = kernel_width // 2
    result = []
    for along_x in range(kernel_width):
        for along_y in range(kernel_width):
            for along_z in range(kernel_width):
                result.append((along_x - middle, along_y - middle, along_z - middle))
    return result


def taps_stack(volume, kernel_width, direction):
    middle = kernel_width // 2
    padded = jnp.pad(volume, ((0, 0), (middle, middle), (middle, middle), (middle, middle)))
    size_x, size_y, size_z = (volume.shape[1], volume.shape[2], volume.shape[3])
    pieces = []
    for off_x, off_y, off_z in tap_offsets(kernel_width):
        start_x = middle + direction * off_x
        start_y = middle + direction * off_y
        start_z = middle + direction * off_z
        pieces.append(
            padded[
                :,
                start_x : start_x + size_x,
                start_y : start_y + size_y,
                start_z : start_z + size_z,
            ]
        )
    stacked = jnp.stack(pieces, 0)
    return stacked.reshape(len(pieces) * volume.shape[0], size_x * size_y * size_z)


def back_input(grad_out, w_rows):
    columns = taps_stack(grad_out, KW, -1)
    summed = lax.dot_general(
        w_rows, columns, (((0,), (0,)), ((), ())), preferred_element_type=jnp.float32
    )
    return summed.astype(jnp.bfloat16).reshape(grad_out.shape)


def back_weight(volume, grad_out):
    columns = taps_stack(volume, KW, 1)
    flattened = grad_out.reshape(grad_out.shape[0], -1)
    return lax.dot_general(
        columns, flattened, (((1,), (1,)), ((), ())), preferred_element_type=jnp.float32
    )


def local_inverse(matrix):
    values = matrix.astype(jnp.float32)
    step_size = 1.0 / jnp.max(jnp.sum(jnp.abs(values), axis=1))
    identity = jnp.eye(matrix.shape[0], dtype=jnp.float32)
    resid0 = (identity - step_size * values).astype(jnp.bfloat16)
    resid1 = jnp.dot(resid0, resid0, preferred_element_type=jnp.float32).astype(jnp.bfloat16)
    cross_term = jnp.dot(resid1, resid0, preferred_element_type=jnp.float32)
    return step_size * (
        identity + resid0.astype(jnp.float32) + resid1.astype(jnp.float32) + cross_term
    )


def eye_rows(start_row, row_total, order_full):
    column_ids = lax.broadcasted_iota(jnp.int32, (row_total, order_full), 1)
    row_ids = lax.broadcasted_iota(jnp.int32, (row_total, order_full), 0)
    return (column_ids == start_row + row_ids).astype(jnp.float32)


def halving_sum(value, axis):
    count = lax.axis_size(axis)
    assert count & (count - 1) == 0 and value.shape[0] % count == 0
    index = lax.axis_index(axis)
    stride = 1
    while stride < count:
        half = value.shape[0] // 2
        upper = (index // stride) % 2 == 1
        keep = jnp.where(upper, value[half:], value[:half])
        send = jnp.where(upper, value[:half], value[half:])
        value = keep + lax.ppermute(send, axis, [(i, i ^ stride) for i in range(count)])
        stride *= 2
    stride = count // 2
    while stride >= 1:
        other = lax.ppermute(value, axis, [(i, i ^ stride) for i in range(count)])
        upper = (index // stride) % 2 == 1
        value = jnp.where(upper, jnp.concatenate([other, value]), jnp.concatenate([value, other]))
        stride //= 2
    return value


def compressed_products(gathered, a_rows, own_eye, shard_count, row_total):
    kept = shard_count // 2 + 1
    order_full = a_rows.shape[1]
    mirrored = shard_count - kept
    magnitudes = jnp.abs(gathered.astype(jnp.float32))
    direct_sums = jnp.sum(jnp.sum(magnitudes, axis=3), axis=1)
    column_sums = jnp.sum(magnitudes, axis=2)
    for offset in range(1, mirrored + 1):
        direct_sums = direct_sums + jnp.roll(column_sums[:, offset], offset, axis=0)
    step_size = 1.0 / jnp.max(direct_sums)
    block_eye = jnp.logical_and(
        lax.broadcasted_iota(jnp.int32, gathered.shape, 1) == 0,
        lax.broadcasted_iota(jnp.int32, gathered.shape, 2)
        == lax.broadcasted_iota(jnp.int32, gathered.shape, 3),
    ).astype(jnp.float32)
    resid_blocks = (block_eye - step_size * gathered.astype(jnp.float32)).astype(jnp.bfloat16)
    direct_right = jnp.stack(
        [jnp.roll(resid_blocks[:, offset], offset, axis=0) for offset in range(kept)], 0
    )
    mirror_right = resid_blocks[:, 1 : mirrored + 1].transpose(1, 0, 2, 3)

    def times_resid0(left_rows):
        left = left_rows.reshape(row_total, shard_count, row_total).transpose(1, 0, 2)
        direct_left = jnp.stack([jnp.roll(left, offset, axis=0) for offset in range(kept)], 0)
        mirror_left = jnp.stack(
            [jnp.roll(left, -offset, axis=0) for offset in range(1, mirrored + 1)], 0
        )
        product = jnp.einsum(
            "kjab,kjbc->jac", direct_left, direct_right, preferred_element_type=jnp.float32
        ) + jnp.einsum(
            "mjab,mjcb->jac", mirror_left, mirror_right, preferred_element_type=jnp.float32
        )
        return product.transpose(1, 0, 2).reshape(row_total, order_full)

    resid0 = (own_eye - step_size * a_rows.astype(jnp.float32)).astype(jnp.bfloat16)
    resid1 = times_resid0(resid0).astype(jnp.bfloat16)
    cross_term = times_resid0(resid1)
    return step_size, resid0, resid1, cross_term


def dense_products(gathered, a_rows, own_eye):
    row_total = a_rows.shape[0]
    shard_count = gathered.shape[0]
    full_values = gathered.astype(jnp.float32)
    step_size = 1.0 / jnp.max(jnp.sum(jnp.abs(full_values), axis=2))
    block_ids = lax.broadcasted_iota(jnp.int32, gathered.shape, 0)
    row_ids = lax.broadcasted_iota(jnp.int32, gathered.shape, 1)
    column_ids = lax.broadcasted_iota(jnp.int32, gathered.shape, 2)
    full_eye = (column_ids == block_ids * row_total + row_ids).astype(jnp.float32)
    full_resid0 = (full_eye - step_size * full_values).astype(jnp.bfloat16)
    contract = (((1, 2), (0, 1)), ((), ()))
    resid0 = (own_eye - step_size * a_rows.astype(jnp.float32)).astype(jnp.bfloat16)
    resid1 = lax.dot_general(
        resid0.reshape(row_total, shard_count, row_total), full_resid0, contract,
        preferred_element_type=jnp.float32,
    ).astype(jnp.bfloat16)
    cross_term = lax.dot_general(
        resid1.reshape(row_total, shard_count, row_total), full_resid0, contract,
        preferred_element_type=jnp.float32,
    )
    return step_size, resid0, resid1, cross_term


def conv_back_input(grad_out, weights_now):
    channels = weights_now.shape[0]
    kernel = weights_now.reshape(channels, KW, KW, KW, channels)[:, ::-1, ::-1, ::-1, :]
    summed = lax.conv_general_dilated(
        grad_out[None], kernel.transpose(4, 0, 1, 2, 3), (1, 1, 1), ((KW // 2, KW // 2),) * 3,
        dimension_numbers=("NCDHW", "OIDHW", "NCDHW"), preferred_element_type=jnp.float32,
    )
    return summed[0].astype(jnp.bfloat16)


def conv_back_weight(volume, grad_out):
    channels = volume.shape[0]
    summed = lax.conv_general_dilated(
        volume[:, None], grad_out[:, None], (1, 1, 1), ((KW // 2, KW // 2),) * 3,
        dimension_numbers=("NCDHW", "OIDHW", "NCDHW"), preferred_element_type=jnp.float32,
    )
    return summed.transpose(2, 3, 4, 0, 1).reshape(KW ** 3 * channels, grad_out.shape[0])


def shards(acts, preacts, top_grad, weights, a_factor, g_factor):
    section_index = lax.axis_index("section")
    section_count = lax.axis_size("section")
    tick_count = MICRO + section_count - 1
    shard_count = lax.axis_size("dp")
    row_total = a_factor.shape[1]
    compressed = shard_count % 2 == 0 and row_total >= 64
    if compressed:
        kept = shard_count // 2 + 1
        own_blocks = a_factor[0].reshape(row_total, shard_count, row_total).transpose(1, 0, 2)
        twice = jnp.concatenate([own_blocks, own_blocks], axis=0)
        upper_blocks = lax.dynamic_slice_in_dim(twice, lax.axis_index("dp"), kept, 0)
        gathered = lax.all_gather(upper_blocks, "dp", axis=0)
    else:
        gathered = lax.all_gather(a_factor[0], "dp", axis=0)
    inputs = acts[0, 0]
    pre_values = preacts[0, 0]
    upper_grads = top_grad[0]
    micro_count = inputs.shape[0]
    zero_field = jnp.zeros(inputs.shape[1:], jnp.bfloat16)
    outgoing = zero_field
    stored_grads = [zero_field] * micro_count
    stored_slopes = [zero_field] * micro_count
    for tick_index in range(micro_count + section_count - 1):
        incoming = shifted(outgoing, "section", -1) if tick_index > 0 else zero_field
        micro_index = tick_index - (section_count - 1 - section_index)
        is_valid = jnp.logical_and(micro_index >= 0, micro_index < micro_count)
        clipped = jnp.clip(micro_index, 0, micro_count - 1)
        from_top = lax.dynamic_index_in_dim(upper_grads, clipped, 0, keepdims=False)
        arriving = jnp.where(section_index == section_count - 1, from_top, incoming)
        pre_now = lax.dynamic_index_in_dim(pre_values, clipped, 0, keepdims=False)
        grad_out = jnp.where(pre_now > 0, arriving, zero_field)
        outgoing = conv_back_input(grad_out, weights[0])
        for micro in range(micro_count):
            keep = jnp.logical_and(is_valid, clipped == micro)
            stored_grads[micro] = jnp.where(keep, outgoing, stored_grads[micro])
            stored_slopes[micro] = jnp.where(keep, grad_out, stored_slopes[micro])
    local_grad = conv_back_weight(inputs[0], stored_slopes[0])
    for micro in range(1, micro_count):
        local_grad = local_grad + conv_back_weight(inputs[micro], stored_slopes[micro])
    stored_grads = jnp.stack(stored_grads, 0)
    summed_grad = halving_sum(local_grad, "dp")
    mean_grad = summed_grad / lax.axis_size("dp")
    a_rows = a_factor[0]
    order_full = a_rows.shape[1]
    first_row = lax.axis_index("dp") * row_total
    own_eye = eye_rows(first_row, row_total, order_full)
    if compressed:
        step_size, resid0, resid1, cross_term = compressed_products(
            gathered, a_rows, own_eye, shard_count, row_total
        )
    else:
        step_size, resid0, resid1, cross_term = dense_products(gathered, a_rows, own_eye)
    inverse_rows = step_size * (
        own_eye + resid0.astype(jnp.float32) + resid1.astype(jnp.float32) + cross_term
    )
    g_inverse = local_inverse(g_factor[0])
    preconditioned = jnp.dot(
        mean_grad, g_inverse, precision=lax.Precision.HIGHEST, preferred_element_type=jnp.float32
    )
    update_rows = jnp.dot(
        inverse_rows,
        preconditioned,
        precision=lax.Precision.HIGHEST,
        preferred_element_type=jnp.float32,
    )
    return (stored_grads[None, None], update_rows[None], inverse_rows[None])


def solution(mesh):
    placed = (
        P("section", "dp", None, None, None, None, None),
        P("section", "dp", None, None, None, None, None),
        P("dp", None, None, None, None, None),
        P("section", None, None),
        P("section", "dp", None),
        P("section", None, None),
    )
    return jax.shard_map(
        shards,
        mesh=mesh,
        in_specs=placed,
        out_specs=(
            P("section", "dp", None, None, None, None, None),
            P("section", "dp", None),
            P("section", "dp", None),
        ),
        check_vma=False,
    )
```

```python
import jax
import numpy as np
import jax.numpy as jnp
from jax import lax
from jax.sharding import PartitionSpec as P

KW = 3
MICRO = 1


def shifted(value, axis, steps):
    count = lax.axis_size(axis)
    first, last = (max(0, -steps), min(count, count - steps))
    return lax.ppermute(value, axis, [(source, source + steps) for source in range(first, last)])


def tap_offsets(kernel_width):
    middle = kernel_width // 2
    result = []
    for along_x in range(kernel_width):
        for along_y in range(kernel_width):
            for along_z in range(kernel_width):
                result.append((along_x - middle, along_y - middle, along_z - middle))
    return result


def taps_stack(volume, kernel_width, direction):
    middle = kernel_width // 2
    padded = jnp.pad(volume, ((0, 0), (middle, middle), (middle, middle), (middle, middle)))
    size_x, size_y, size_z = (volume.shape[1], volume.shape[2], volume.shape[3])
    pieces = []
    for off_x, off_y, off_z in tap_offsets(kernel_width):
        start_x = middle + direction * off_x
        start_y = middle + direction * off_y
        start_z = middle + direction * off_z
        pieces.append(
            padded[
                :,
                start_x : start_x + size_x,
                start_y : start_y + size_y,
                start_z : start_z + size_z,
            ]
        )
    stacked = jnp.stack(pieces, 0)
    return stacked.reshape(len(pieces) * volume.shape[0], size_x * size_y * size_z)


def back_input(grad_out, w_rows):
    columns = taps_stack(grad_out, KW, -1)
    summed = lax.dot_general(
        w_rows, columns, (((0,), (0,)), ((), ())), preferred_element_type=jnp.float32
    )
    return summed.astype(jnp.bfloat16).reshape(grad_out.shape)


def back_weight(volume, grad_out):
    columns = taps_stack(volume, KW, 1)
    flattened = grad_out.reshape(grad_out.shape[0], -1)
    return lax.dot_general(
        columns, flattened, (((1,), (1,)), ((), ())), preferred_element_type=jnp.float32
    )


def local_inverse(matrix):
    values = matrix.astype(jnp.float32)
    step_size = 1.0 / jnp.max(jnp.sum(jnp.abs(values), axis=1))
    identity = jnp.eye(matrix.shape[0], dtype=jnp.float32)
    resid0 = (identity - step_size * values).astype(jnp.bfloat16)
    resid1 = jnp.dot(resid0, resid0, preferred_element_type=jnp.float32).astype(jnp.bfloat16)
    cross_term = jnp.dot(resid1, resid0, preferred_element_type=jnp.float32)
    return step_size * (
        identity + resid0.astype(jnp.float32) + resid1.astype(jnp.float32) + cross_term
    )


def eye_rows(start_row, row_total, order_full):
    column_ids = lax.broadcasted_iota(jnp.int32, (row_total, order_full), 1)
    row_ids = lax.broadcasted_iota(jnp.int32, (row_total, order_full), 0)
    return (column_ids == start_row + row_ids).astype(jnp.float32)


def halving_sum(value, axis):
    count = lax.axis_size(axis)
    assert count & (count - 1) == 0 and value.shape[0] % count == 0
    index = lax.axis_index(axis)
    stride = 1
    while stride < count:
        half = value.shape[0] // 2
        upper = (index // stride) % 2 == 1
        keep = jnp.where(upper, value[half:], value[:half])
        send = jnp.where(upper, value[:half], value[half:])
        value = keep + lax.ppermute(send, axis, [(i, i ^ stride) for i in range(count)])
        stride *= 2
    stride = count // 2
    while stride >= 1:
        other = lax.ppermute(value, axis, [(i, i ^ stride) for i in range(count)])
        upper = (index // stride) % 2 == 1
        value = jnp.where(upper, jnp.concatenate([other, value]), jnp.concatenate([value, other]))
        stride //= 2
    return value


def compressed_products(gathered, a_rows, own_eye, shard_count, row_total, step_size):
    kept = shard_count // 2 + 1
    order_full = a_rows.shape[1]
    mirrored = shard_count - kept
    block_eye = jnp.logical_and(
        lax.broadcasted_iota(jnp.int32, gathered.shape, 1) == 0,
        lax.broadcasted_iota(jnp.int32, gathered.shape, 2)
        == lax.broadcasted_iota(jnp.int32, gathered.shape, 3),
    ).astype(jnp.float32)
    resid_blocks = (block_eye - step_size * gathered.astype(jnp.float32)).astype(jnp.bfloat16)
    columns = np.arange(shard_count)[None, :]
    direct_index = (columns - np.arange(kept)[:, None]) % shard_count
    mirror_index = (columns + np.arange(1, mirrored + 1)[:, None]) % shard_count
    direct_right = resid_blocks[direct_index, np.arange(kept)[:, None]]
    mirror_right = resid_blocks[:, 1 : mirrored + 1].transpose(1, 0, 2, 3)

    def times_resid0(left):
        return jnp.einsum(
            "kjab,kjbc->jac", left[direct_index], direct_right, preferred_element_type=jnp.float32
        ) + jnp.einsum(
            "mjab,mjcb->jac", left[mirror_index], mirror_right, preferred_element_type=jnp.float32
        )

    def as_blocks(rows):
        return rows.reshape(row_total, shard_count, row_total).transpose(1, 0, 2)

    resid0 = (own_eye - step_size * a_rows.astype(jnp.float32)).astype(jnp.bfloat16)
    resid1 = times_resid0(as_blocks(resid0)).astype(jnp.bfloat16)
    cross_term = times_resid0(resid1)
    total = (
        as_blocks(own_eye) + as_blocks(resid0).astype(jnp.float32) + resid1.astype(jnp.float32)
        + cross_term
    )
    return (step_size * total).transpose(1, 0, 2).reshape(row_total, order_full)


def largest(value, axis):
    count = lax.axis_size(axis)
    stride = 1
    while stride < count:
        value = jnp.maximum(value, lax.ppermute(value, axis, [(i, i ^ stride) for i in range(count)]))
        stride *= 2
    return value


def dense_products(gathered, a_rows, own_eye):
    row_total = a_rows.shape[0]
    shard_count = gathered.shape[0]
    full_values = gathered.astype(jnp.float32)
    step_size = 1.0 / jnp.max(jnp.sum(jnp.abs(full_values), axis=2))
    block_ids = lax.broadcasted_iota(jnp.int32, gathered.shape, 0)
    row_ids = lax.broadcasted_iota(jnp.int32, gathered.shape, 1)
    column_ids = lax.broadcasted_iota(jnp.int32, gathered.shape, 2)
    full_eye = (column_ids == block_ids * row_total + row_ids).astype(jnp.float32)
    full_resid0 = (full_eye - step_size * full_values).astype(jnp.bfloat16)
    contract = (((1, 2), (0, 1)), ((), ()))
    resid0 = (own_eye - step_size * a_rows.astype(jnp.float32)).astype(jnp.bfloat16)
    resid1 = lax.dot_general(
        resid0.reshape(row_total, shard_count, row_total), full_resid0, contract,
        preferred_element_type=jnp.float32,
    ).astype(jnp.bfloat16)
    cross_term = lax.dot_general(
        resid1.reshape(row_total, shard_count, row_total), full_resid0, contract,
        preferred_element_type=jnp.float32,
    )
    return step_size, resid0, resid1, cross_term


def conv_back_input(grad_out, weights_now):
    channels = weights_now.shape[0]
    kernel = weights_now.reshape(channels, KW, KW, KW, channels)[:, ::-1, ::-1, ::-1, :]
    summed = lax.conv_general_dilated(
        grad_out[None], kernel.transpose(4, 0, 1, 2, 3), (1, 1, 1), ((KW // 2, KW // 2),) * 3,
        dimension_numbers=("NCDHW", "OIDHW", "NCDHW"), preferred_element_type=jnp.float32,
    )
    return summed[0].astype(jnp.bfloat16)


def conv_back_weight(volume, grad_out):
    channels = volume.shape[0]
    summed = lax.conv_general_dilated(
        volume[:, None], grad_out[:, None], (1, 1, 1), ((KW // 2, KW // 2),) * 3,
        dimension_numbers=("NCDHW", "OIDHW", "NCDHW"), preferred_element_type=jnp.float32,
    )
    return summed.transpose(2, 3, 4, 0, 1).reshape(KW ** 3 * channels, grad_out.shape[0])


def shards(acts, preacts, top_grad, weights, a_factor, g_factor):
    section_index = lax.axis_index("section")
    section_count = lax.axis_size("section")
    tick_count = MICRO + section_count - 1
    shard_count = lax.axis_size("dp")
    row_total = a_factor.shape[1]
    compressed = shard_count % 2 == 0 and row_total >= 64
    if compressed:
        kept = shard_count // 2 + 1
        own_blocks = a_factor[0].reshape(row_total, shard_count, row_total).transpose(1, 0, 2)
        twice = jnp.concatenate([own_blocks, own_blocks], axis=0)
        upper_blocks = lax.dynamic_slice_in_dim(twice, lax.axis_index("dp"), kept, 0)
        gathered = lax.all_gather(upper_blocks, "dp", axis=0)
        local_largest = jnp.max(jnp.sum(jnp.abs(a_factor[0].astype(jnp.float32)), axis=1))
        step_size = 1.0 / largest(local_largest, "dp")
    else:
        gathered = lax.all_gather(a_factor[0], "dp", axis=0)
    inputs = acts[0, 0]
    pre_values = preacts[0, 0]
    upper_grads = top_grad[0]
    micro_count = inputs.shape[0]
    zero_field = jnp.zeros(inputs.shape[1:], jnp.bfloat16)
    outgoing = zero_field
    stored_grads = [zero_field] * micro_count
    stored_slopes = [zero_field] * micro_count
    for tick_index in range(micro_count + section_count - 1):
        incoming = shifted(outgoing, "section", -1) if tick_index > 0 else zero_field
        micro_index = tick_index - (section_count - 1 - section_index)
        is_valid = jnp.logical_and(micro_index >= 0, micro_index < micro_count)
        clipped = jnp.clip(micro_index, 0, micro_count - 1)
        from_top = lax.dynamic_index_in_dim(upper_grads, clipped, 0, keepdims=False)
        arriving = jnp.where(section_index == section_count - 1, from_top, incoming)
        pre_now = lax.dynamic_index_in_dim(pre_values, clipped, 0, keepdims=False)
        grad_out = jnp.where(pre_now > 0, arriving, zero_field)
        outgoing = conv_back_input(grad_out, weights[0])
        for micro in range(micro_count):
            keep = jnp.logical_and(is_valid, clipped == micro)
            stored_grads[micro] = jnp.where(keep, outgoing, stored_grads[micro])
            stored_slopes[micro] = jnp.where(keep, grad_out, stored_slopes[micro])
    local_grad = conv_back_weight(inputs[0], stored_slopes[0])
    for micro in range(1, micro_count):
        local_grad = local_grad + conv_back_weight(inputs[micro], stored_slopes[micro])
    stored_grads = jnp.stack(stored_grads, 0)
    summed_grad = halving_sum(local_grad, "dp")
    mean_grad = summed_grad / lax.axis_size("dp")
    a_rows = a_factor[0]
    order_full = a_rows.shape[1]
    first_row = lax.axis_index("dp") * row_total
    own_eye = eye_rows(first_row, row_total, order_full)
    if compressed:
        inverse_rows = compressed_products(
            gathered, a_rows, own_eye, shard_count, row_total, step_size
        )
    else:
        step_size, resid0, resid1, cross_term = dense_products(gathered, a_rows, own_eye)
        inverse_rows = step_size * (
            own_eye + resid0.astype(jnp.float32) + resid1.astype(jnp.float32) + cross_term
        )
    g_inverse = local_inverse(g_factor[0])
    preconditioned = jnp.dot(
        mean_grad, g_inverse, precision=lax.Precision.HIGHEST, preferred_element_type=jnp.float32
    )
    update_rows = jnp.dot(
        inverse_rows,
        preconditioned,
        precision=lax.Precision.HIGHEST,
        preferred_element_type=jnp.float32,
    )
    return (stored_grads[None, None], update_rows[None], inverse_rows[None])


def solution(mesh):
    placed = (
        P("section", "dp", None, None, None, None, None),
        P("section", "dp", None, None, None, None, None),
        P("dp", None, None, None, None, None),
        P("section", None, None),
        P("section", "dp", None),
        P("section", None, None),
    )
    return jax.shard_map(
        shards,
        mesh=mesh,
        in_specs=placed,
        out_specs=(
            P("section", "dp", None, None, None, None, None),
            P("section", "dp", None),
            P("section", "dp", None),
        ),
        check_vma=False,
    )
```

```python
import jax
import jax.numpy as jnp
from jax import lax
from jax.sharding import PartitionSpec as P

KW = 3
MICRO = 1


def shifted(value, axis, steps):
    count = lax.axis_size(axis)
    first, last = (max(0, -steps), min(count, count - steps))
    return lax.ppermute(value, axis, [(source, source + steps) for source in range(first, last)])


def tap_offsets(kernel_width):
    middle = kernel_width // 2
    result = []
    for along_x in range(kernel_width):
        for along_y in range(kernel_width):
            for along_z in range(kernel_width):
                result.append((along_x - middle, along_y - middle, along_z - middle))
    return result


def taps_stack(volume, kernel_width, direction):
    middle = kernel_width // 2
    padded = jnp.pad(volume, ((0, 0), (middle, middle), (middle, middle), (middle, middle)))
    size_x, size_y, size_z = (volume.shape[1], volume.shape[2], volume.shape[3])
    pieces = []
    for off_x, off_y, off_z in tap_offsets(kernel_width):
        start_x = middle + direction * off_x
        start_y = middle + direction * off_y
        start_z = middle + direction * off_z
        pieces.append(
            padded[
                :,
                start_x : start_x + size_x,
                start_y : start_y + size_y,
                start_z : start_z + size_z,
            ]
        )
    stacked = jnp.stack(pieces, 0)
    return stacked.reshape(len(pieces) * volume.shape[0], size_x * size_y * size_z)


def back_input(grad_out, w_rows):
    columns = taps_stack(grad_out, KW, -1)
    summed = lax.dot_general(
        w_rows, columns, (((0,), (0,)), ((), ())), preferred_element_type=jnp.float32
    )
    return summed.astype(jnp.bfloat16).reshape(grad_out.shape)


def back_weight(volume, grad_out):
    columns = taps_stack(volume, KW, 1)
    flattened = grad_out.reshape(grad_out.shape[0], -1)
    return lax.dot_general(
        columns, flattened, (((1,), (1,)), ((), ())), preferred_element_type=jnp.float32
    )


def local_inverse(matrix):
    values = matrix.astype(jnp.float32)
    step_size = 1.0 / jnp.max(jnp.sum(jnp.abs(values), axis=1))
    identity = jnp.eye(matrix.shape[0], dtype=jnp.float32)
    resid0 = (identity - step_size * values).astype(jnp.bfloat16)
    resid1 = jnp.dot(resid0, resid0, preferred_element_type=jnp.float32).astype(jnp.bfloat16)
    cross_term = jnp.dot(resid1, resid0, preferred_element_type=jnp.float32)
    return step_size * (
        identity + resid0.astype(jnp.float32) + resid1.astype(jnp.float32) + cross_term
    )


def eye_rows(start_row, row_total, order_full):
    column_ids = lax.broadcasted_iota(jnp.int32, (row_total, order_full), 1)
    row_ids = lax.broadcasted_iota(jnp.int32, (row_total, order_full), 0)
    return (column_ids == start_row + row_ids).astype(jnp.float32)


def halving_sum(value, axis):
    count = lax.axis_size(axis)
    assert count & (count - 1) == 0 and value.shape[0] % count == 0
    index = lax.axis_index(axis)
    stride = 1
    while stride < count:
        half = value.shape[0] // 2
        upper = (index // stride) % 2 == 1
        keep = jnp.where(upper, value[half:], value[:half])
        send = jnp.where(upper, value[:half], value[half:])
        value = keep + lax.ppermute(send, axis, [(i, i ^ stride) for i in range(count)])
        stride *= 2
    stride = count // 2
    while stride >= 1:
        other = lax.ppermute(value, axis, [(i, i ^ stride) for i in range(count)])
        upper = (index // stride) % 2 == 1
        value = jnp.where(upper, jnp.concatenate([other, value]), jnp.concatenate([value, other]))
        stride //= 2
    return value


def compressed_products(gathered, a_rows, own_eye, shard_count, row_total):
    kept = shard_count // 2 + 1
    order_full = a_rows.shape[1]
    mirrored = shard_count - kept
    magnitudes = jnp.abs(gathered.astype(jnp.float32))
    direct_sums = jnp.sum(jnp.sum(magnitudes, axis=3), axis=1)
    column_sums = jnp.sum(magnitudes, axis=2)
    for offset in range(1, mirrored + 1):
        direct_sums = direct_sums + jnp.roll(column_sums[:, offset], offset, axis=0)
    step_size = 1.0 / jnp.max(direct_sums)
    block_eye = jnp.logical_and(
        lax.broadcasted_iota(jnp.int32, gathered.shape, 1) == 0,
        lax.broadcasted_iota(jnp.int32, gathered.shape, 2)
        == lax.broadcasted_iota(jnp.int32, gathered.shape, 3),
    ).astype(jnp.float32)
    resid_blocks = (block_eye - step_size * gathered.astype(jnp.float32)).astype(jnp.bfloat16)
    doubled_right = jnp.concatenate([resid_blocks, resid_blocks], axis=0)
    direct_right = jnp.stack(
        [doubled_right[shard_count - offset : 2 * shard_count - offset, offset] for offset in range(kept)], 0
    )
    mirror_right = resid_blocks[:, 1 : mirrored + 1].transpose(1, 0, 2, 3)

    def times_resid0(left_rows):
        left = left_rows.reshape(row_total, shard_count, row_total).transpose(1, 0, 2)
        doubled = jnp.concatenate([left, left], axis=0)
        direct_left = jnp.stack(
            [doubled[shard_count - offset : 2 * shard_count - offset] for offset in range(kept)], 0
        )
        mirror_left = jnp.stack(
            [doubled[offset : shard_count + offset] for offset in range(1, mirrored + 1)], 0
        )
        product = jnp.einsum(
            "kjab,kjbc->jac", direct_left, direct_right, preferred_element_type=jnp.float32
        ) + jnp.einsum(
            "mjab,mjcb->jac", mirror_left, mirror_right, preferred_element_type=jnp.float32
        )
        return product.transpose(1, 0, 2).reshape(row_total, order_full)

    resid0 = (own_eye - step_size * a_rows.astype(jnp.float32)).astype(jnp.bfloat16)
    resid1 = times_resid0(resid0).astype(jnp.bfloat16)
    cross_term = times_resid0(resid1)
    return step_size, resid0, resid1, cross_term


def dense_products(gathered, a_rows, own_eye):
    row_total = a_rows.shape[0]
    shard_count = gathered.shape[0]
    full_values = gathered.astype(jnp.float32)
    step_size = 1.0 / jnp.max(jnp.sum(jnp.abs(full_values), axis=2))
    block_ids = lax.broadcasted_iota(jnp.int32, gathered.shape, 0)
    row_ids = lax.broadcasted_iota(jnp.int32, gathered.shape, 1)
    column_ids = lax.broadcasted_iota(jnp.int32, gathered.shape, 2)
    full_eye = (column_ids == block_ids * row_total + row_ids).astype(jnp.float32)
    full_resid0 = (full_eye - step_size * full_values).astype(jnp.bfloat16)
    contract = (((1, 2), (0, 1)), ((), ()))
    resid0 = (own_eye - step_size * a_rows.astype(jnp.float32)).astype(jnp.bfloat16)
    resid1 = lax.dot_general(
        resid0.reshape(row_total, shard_count, row_total), full_resid0, contract,
        preferred_element_type=jnp.float32,
    ).astype(jnp.bfloat16)
    cross_term = lax.dot_general(
        resid1.reshape(row_total, shard_count, row_total), full_resid0, contract,
        preferred_element_type=jnp.float32,
    )
    return step_size, resid0, resid1, cross_term


def conv_back_input(grad_out, weights_now):
    channels = weights_now.shape[0]
    kernel = weights_now.reshape(channels, KW, KW, KW, channels)[:, ::-1, ::-1, ::-1, :]
    summed = lax.conv_general_dilated(
        grad_out[None], kernel.transpose(4, 0, 1, 2, 3), (1, 1, 1), ((KW // 2, KW // 2),) * 3,
        dimension_numbers=("NCDHW", "OIDHW", "NCDHW"), preferred_element_type=jnp.float32,
    )
    return summed[0].astype(jnp.bfloat16)


def conv_back_weight(volume, grad_out):
    channels = volume.shape[0]
    summed = lax.conv_general_dilated(
        volume[:, None], grad_out[:, None], (1, 1, 1), ((KW // 2, KW // 2),) * 3,
        dimension_numbers=("NCDHW", "OIDHW", "NCDHW"), preferred_element_type=jnp.float32,
    )
    return summed.transpose(2, 3, 4, 0, 1).reshape(KW ** 3 * channels, grad_out.shape[0])


def shards(acts, preacts, top_grad, weights, a_factor, g_factor):
    section_index = lax.axis_index("section")
    section_count = lax.axis_size("section")
    tick_count = MICRO + section_count - 1
    shard_count = lax.axis_size("dp")
    row_total = a_factor.shape[1]
    compressed = shard_count % 2 == 0 and row_total >= 64
    if compressed:
        kept = shard_count // 2 + 1
        own_blocks = a_factor[0].reshape(row_total, shard_count, row_total).transpose(1, 0, 2)
        twice = jnp.concatenate([own_blocks, own_blocks], axis=0)
        upper_blocks = lax.dynamic_slice_in_dim(twice, lax.axis_index("dp"), kept, 0)
        gathered = lax.all_gather(upper_blocks, "dp", axis=0)
    else:
        gathered = lax.all_gather(a_factor[0], "dp", axis=0)
    inputs = acts[0, 0]
    pre_values = preacts[0, 0]
    upper_grads = top_grad[0]
    micro_count = inputs.shape[0]
    zero_field = jnp.zeros(inputs.shape[1:], jnp.bfloat16)
    outgoing = zero_field
    stored_grads = [zero_field] * micro_count
    stored_slopes = [zero_field] * micro_count
    for tick_index in range(micro_count + section_count - 1):
        incoming = shifted(outgoing, "section", -1) if tick_index > 0 else zero_field
        micro_index = tick_index - (section_count - 1 - section_index)
        is_valid = jnp.logical_and(micro_index >= 0, micro_index < micro_count)
        clipped = jnp.clip(micro_index, 0, micro_count - 1)
        from_top = lax.dynamic_index_in_dim(upper_grads, clipped, 0, keepdims=False)
        arriving = jnp.where(section_index == section_count - 1, from_top, incoming)
        pre_now = lax.dynamic_index_in_dim(pre_values, clipped, 0, keepdims=False)
        grad_out = jnp.where(pre_now > 0, arriving, zero_field)
        outgoing = conv_back_input(grad_out, weights[0])
        for micro in range(micro_count):
            keep = jnp.logical_and(is_valid, clipped == micro)
            stored_grads[micro] = jnp.where(keep, outgoing, stored_grads[micro])
            stored_slopes[micro] = jnp.where(keep, grad_out, stored_slopes[micro])
    local_grad = conv_back_weight(inputs[0], stored_slopes[0])
    for micro in range(1, micro_count):
        local_grad = local_grad + conv_back_weight(inputs[micro], stored_slopes[micro])
    stored_grads = jnp.stack(stored_grads, 0)
    summed_grad = halving_sum(local_grad, "dp")
    mean_grad = summed_grad / lax.axis_size("dp")
    a_rows = a_factor[0]
    order_full = a_rows.shape[1]
    first_row = lax.axis_index("dp") * row_total
    own_eye = eye_rows(first_row, row_total, order_full)
    if compressed:
        step_size, resid0, resid1, cross_term = compressed_products(
            gathered, a_rows, own_eye, shard_count, row_total
        )
    else:
        step_size, resid0, resid1, cross_term = dense_products(gathered, a_rows, own_eye)
    inverse_rows = step_size * (
        own_eye + resid0.astype(jnp.float32) + resid1.astype(jnp.float32) + cross_term
    )
    g_inverse = local_inverse(g_factor[0])
    preconditioned = jnp.dot(
        mean_grad, g_inverse, precision=lax.Precision.HIGHEST, preferred_element_type=jnp.float32
    )
    update_rows = jnp.dot(
        inverse_rows,
        preconditioned,
        precision=lax.Precision.HIGHEST,
        preferred_element_type=jnp.float32,
    )
    return (stored_grads[None, None], update_rows[None], inverse_rows[None])


def solution(mesh):
    placed = (
        P("section", "dp", None, None, None, None, None),
        P("section", "dp", None, None, None, None, None),
        P("dp", None, None, None, None, None),
        P("section", None, None),
        P("section", "dp", None),
        P("section", None, None),
    )
    return jax.shard_map(
        shards,
        mesh=mesh,
        in_specs=placed,
        out_specs=(
            P("section", "dp", None, None, None, None, None),
            P("section", "dp", None),
            P("section", "dp", None),
        ),
        check_vma=False,
    )
```

```python
import jax
import jax.numpy as jnp
from jax import lax
from jax.sharding import PartitionSpec as P

KW = 3
MICRO = 1


def shifted(value, axis, steps):
    count = lax.axis_size(axis)
    first, last = (max(0, -steps), min(count, count - steps))
    return lax.ppermute(value, axis, [(source, source + steps) for source in range(first, last)])


def tap_offsets(kernel_width):
    middle = kernel_width // 2
    result = []
    for along_x in range(kernel_width):
        for along_y in range(kernel_width):
            for along_z in range(kernel_width):
                result.append((along_x - middle, along_y - middle, along_z - middle))
    return result


def taps_stack(volume, kernel_width, direction):
    middle = kernel_width // 2
    padded = jnp.pad(volume, ((0, 0), (middle, middle), (middle, middle), (middle, middle)))
    size_x, size_y, size_z = (volume.shape[1], volume.shape[2], volume.shape[3])
    pieces = []
    for off_x, off_y, off_z in tap_offsets(kernel_width):
        start_x = middle + direction * off_x
        start_y = middle + direction * off_y
        start_z = middle + direction * off_z
        pieces.append(
            padded[
                :,
                start_x : start_x + size_x,
                start_y : start_y + size_y,
                start_z : start_z + size_z,
            ]
        )
    stacked = jnp.stack(pieces, 0)
    return stacked.reshape(len(pieces) * volume.shape[0], size_x * size_y * size_z)


def back_input(grad_out, w_rows):
    columns = taps_stack(grad_out, KW, -1)
    summed = lax.dot_general(
        w_rows, columns, (((0,), (0,)), ((), ())), preferred_element_type=jnp.float32
    )
    return summed.astype(jnp.bfloat16).reshape(grad_out.shape)


def back_weight(volume, grad_out):
    columns = taps_stack(volume, KW, 1)
    flattened = grad_out.reshape(grad_out.shape[0], -1)
    return lax.dot_general(
        columns, flattened, (((1,), (1,)), ((), ())), preferred_element_type=jnp.float32
    )


def local_inverse(matrix):
    values = matrix.astype(jnp.float32)
    step_size = 1.0 / jnp.max(jnp.sum(jnp.abs(values), axis=1))
    identity = jnp.eye(matrix.shape[0], dtype=jnp.float32)
    resid0 = (identity - step_size * values).astype(jnp.bfloat16)
    resid1 = jnp.dot(resid0, resid0, preferred_element_type=jnp.float32).astype(jnp.bfloat16)
    cross_term = jnp.dot(resid1, resid0, preferred_element_type=jnp.float32)
    return step_size * (
        identity + resid0.astype(jnp.float32) + resid1.astype(jnp.float32) + cross_term
    )


def eye_rows(start_row, row_total, order_full):
    column_ids = lax.broadcasted_iota(jnp.int32, (row_total, order_full), 1)
    row_ids = lax.broadcasted_iota(jnp.int32, (row_total, order_full), 0)
    return (column_ids == start_row + row_ids).astype(jnp.float32)


def halving_sum(value, axis, extra=None):
    count = lax.axis_size(axis)
    assert count & (count - 1) == 0 and value.shape[0] % count == 0
    index = lax.axis_index(axis)
    stride = 1
    while stride < count:
        half = value.shape[0] // 2
        upper = (index // stride) % 2 == 1
        keep = jnp.where(upper, value[half:], value[:half])
        send = jnp.where(upper, value[:half], value[half:])
        value = keep + lax.ppermute(send, axis, [(i, i ^ stride) for i in range(count)])
        stride *= 2
    if extra is not None:
        value = jnp.concatenate([value, extra], axis=0)
    stride = count // 2
    while stride >= 1:
        other = lax.ppermute(value, axis, [(i, i ^ stride) for i in range(count)])
        upper = (index // stride) % 2 == 1
        value = jnp.where(upper, jnp.concatenate([other, value]), jnp.concatenate([value, other]))
        stride //= 2
    if extra is None:
        return value
    pieces = value.reshape(count, -1, value.shape[1])
    held = pieces.shape[1] - extra.shape[0]
    return pieces[:, :held].reshape(-1, value.shape[1]), pieces[:, held:]


def compressed_products(gathered, a_rows, own_eye, shard_count, row_total, step_size):
    kept = shard_count // 2 + 1
    order_full = a_rows.shape[1]
    mirrored = shard_count - kept
    block_eye = jnp.logical_and(
        lax.broadcasted_iota(jnp.int32, gathered.shape, 1) == 0,
        lax.broadcasted_iota(jnp.int32, gathered.shape, 2)
        == lax.broadcasted_iota(jnp.int32, gathered.shape, 3),
    ).astype(jnp.float32)
    resid_blocks = (block_eye - step_size * gathered.astype(jnp.float32)).astype(jnp.bfloat16)
    doubled_right = jnp.concatenate([resid_blocks, resid_blocks], axis=0)
    direct_right = jnp.stack(
        [doubled_right[shard_count - offset : 2 * shard_count - offset, offset] for offset in range(kept)], 0
    )
    mirror_right = resid_blocks[:, 1 : mirrored + 1].transpose(1, 0, 2, 3)

    def times_resid0(left_rows):
        left = left_rows.reshape(row_total, shard_count, row_total).transpose(1, 0, 2)
        doubled = jnp.concatenate([left, left], axis=0)
        direct_left = jnp.stack(
            [doubled[shard_count - offset : 2 * shard_count - offset] for offset in range(kept)], 0
        )
        mirror_left = jnp.stack(
            [doubled[offset : shard_count + offset] for offset in range(1, mirrored + 1)], 0
        )
        product = jnp.einsum(
            "kjab,kjbc->jac", direct_left, direct_right, preferred_element_type=jnp.float32
        ) + jnp.einsum(
            "mjab,mjcb->jac", mirror_left, mirror_right, preferred_element_type=jnp.float32
        )
        return product.transpose(1, 0, 2).reshape(row_total, order_full)

    resid0 = (own_eye - step_size * a_rows.astype(jnp.float32)).astype(jnp.bfloat16)
    resid1 = times_resid0(resid0).astype(jnp.bfloat16)
    cross_term = times_resid0(resid1)
    return resid0, resid1, cross_term


def dense_products(gathered, a_rows, own_eye):
    row_total = a_rows.shape[0]
    shard_count = gathered.shape[0]
    full_values = gathered.astype(jnp.float32)
    step_size = 1.0 / jnp.max(jnp.sum(jnp.abs(full_values), axis=2))
    block_ids = lax.broadcasted_iota(jnp.int32, gathered.shape, 0)
    row_ids = lax.broadcasted_iota(jnp.int32, gathered.shape, 1)
    column_ids = lax.broadcasted_iota(jnp.int32, gathered.shape, 2)
    full_eye = (column_ids == block_ids * row_total + row_ids).astype(jnp.float32)
    full_resid0 = (full_eye - step_size * full_values).astype(jnp.bfloat16)
    contract = (((1, 2), (0, 1)), ((), ()))
    resid0 = (own_eye - step_size * a_rows.astype(jnp.float32)).astype(jnp.bfloat16)
    resid1 = lax.dot_general(
        resid0.reshape(row_total, shard_count, row_total), full_resid0, contract,
        preferred_element_type=jnp.float32,
    ).astype(jnp.bfloat16)
    cross_term = lax.dot_general(
        resid1.reshape(row_total, shard_count, row_total), full_resid0, contract,
        preferred_element_type=jnp.float32,
    )
    return step_size, resid0, resid1, cross_term


def conv_back_input(grad_out, weights_now):
    channels = weights_now.shape[0]
    kernel = weights_now.reshape(channels, KW, KW, KW, channels)[:, ::-1, ::-1, ::-1, :]
    summed = lax.conv_general_dilated(
        grad_out[None], kernel.transpose(4, 0, 1, 2, 3), (1, 1, 1), ((KW // 2, KW // 2),) * 3,
        dimension_numbers=("NCDHW", "OIDHW", "NCDHW"), preferred_element_type=jnp.float32,
    )
    return summed[0].astype(jnp.bfloat16)


def conv_back_weight(volume, grad_out):
    channels = volume.shape[0]
    summed = lax.conv_general_dilated(
        volume[:, None], grad_out[:, None], (1, 1, 1), ((KW // 2, KW // 2),) * 3,
        dimension_numbers=("NCDHW", "OIDHW", "NCDHW"), preferred_element_type=jnp.float32,
    )
    return summed.transpose(2, 3, 4, 0, 1).reshape(KW ** 3 * channels, grad_out.shape[0])


def shards(acts, preacts, top_grad, weights, a_factor, g_factor):
    section_index = lax.axis_index("section")
    section_count = lax.axis_size("section")
    tick_count = MICRO + section_count - 1
    shard_count = lax.axis_size("dp")
    row_total = a_factor.shape[1]
    compressed = shard_count % 2 == 0 and row_total >= 64
    if compressed:
        kept = shard_count // 2 + 1
        own_blocks = a_factor[0].reshape(row_total, shard_count, row_total).transpose(1, 0, 2)
        twice = jnp.concatenate([own_blocks, own_blocks], axis=0)
        upper_blocks = lax.dynamic_slice_in_dim(twice, lax.axis_index("dp"), kept, 0)
        gathered = lax.all_gather(upper_blocks, "dp", axis=0)
    else:
        gathered = lax.all_gather(a_factor[0], "dp", axis=0)
    inputs = acts[0, 0]
    pre_values = preacts[0, 0]
    upper_grads = top_grad[0]
    micro_count = inputs.shape[0]
    zero_field = jnp.zeros(inputs.shape[1:], jnp.bfloat16)
    outgoing = zero_field
    stored_grads = [zero_field] * micro_count
    stored_slopes = [zero_field] * micro_count
    for tick_index in range(micro_count + section_count - 1):
        incoming = shifted(outgoing, "section", -1) if tick_index > 0 else zero_field
        micro_index = tick_index - (section_count - 1 - section_index)
        is_valid = jnp.logical_and(micro_index >= 0, micro_index < micro_count)
        clipped = jnp.clip(micro_index, 0, micro_count - 1)
        from_top = lax.dynamic_index_in_dim(upper_grads, clipped, 0, keepdims=False)
        arriving = jnp.where(section_index == section_count - 1, from_top, incoming)
        pre_now = lax.dynamic_index_in_dim(pre_values, clipped, 0, keepdims=False)
        grad_out = jnp.where(pre_now > 0, arriving, zero_field)
        outgoing = conv_back_input(grad_out, weights[0])
        for micro in range(micro_count):
            keep = jnp.logical_and(is_valid, clipped == micro)
            stored_grads[micro] = jnp.where(keep, outgoing, stored_grads[micro])
            stored_slopes[micro] = jnp.where(keep, grad_out, stored_slopes[micro])
    local_grad = conv_back_weight(inputs[0], stored_slopes[0])
    for micro in range(1, micro_count):
        local_grad = local_grad + conv_back_weight(inputs[micro], stored_slopes[micro])
    stored_grads = jnp.stack(stored_grads, 0)
    if compressed:
        local_largest = jnp.max(jnp.sum(jnp.abs(a_factor[0].astype(jnp.float32)), axis=1))
        carried = jnp.zeros((1, local_grad.shape[1]), jnp.float32).at[0, 0].set(local_largest)
        summed_grad, carried = halving_sum(local_grad, "dp", carried)
        step_size = 1.0 / jnp.max(carried[:, 0, 0])
    else:
        summed_grad = halving_sum(local_grad, "dp")
    mean_grad = summed_grad / lax.axis_size("dp")
    a_rows = a_factor[0]
    order_full = a_rows.shape[1]
    first_row = lax.axis_index("dp") * row_total
    own_eye = eye_rows(first_row, row_total, order_full)
    if compressed:
        resid0, resid1, cross_term = compressed_products(
            gathered, a_rows, own_eye, shard_count, row_total, step_size
        )
    else:
        step_size, resid0, resid1, cross_term = dense_products(gathered, a_rows, own_eye)
    inverse_rows = step_size * (
        own_eye + resid0.astype(jnp.float32) + resid1.astype(jnp.float32) + cross_term
    )
    g_inverse = local_inverse(g_factor[0])
    preconditioned = jnp.dot(
        mean_grad, g_inverse, precision=lax.Precision.HIGHEST, preferred_element_type=jnp.float32
    )
    update_rows = jnp.dot(
        inverse_rows,
        preconditioned,
        precision=lax.Precision.HIGHEST,
        preferred_element_type=jnp.float32,
    )
    return (stored_grads[None, None], update_rows[None], inverse_rows[None])


def solution(mesh):
    placed = (
        P("section", "dp", None, None, None, None, None),
        P("section", "dp", None, None, None, None, None),
        P("dp", None, None, None, None, None),
        P("section", None, None),
        P("section", "dp", None),
        P("section", None, None),
    )
    return jax.shard_map(
        shards,
        mesh=mesh,
        in_specs=placed,
        out_specs=(
            P("section", "dp", None, None, None, None, None),
            P("section", "dp", None),
            P("section", "dp", None),
        ),
        check_vma=False,
    )
```

```python
import jax
import jax.numpy as jnp
from jax import lax
from jax.sharding import PartitionSpec as P

KW = 3
MICRO = 1


def shifted(value, axis, steps):
    count = lax.axis_size(axis)
    first, last = (max(0, -steps), min(count, count - steps))
    return lax.ppermute(value, axis, [(source, source + steps) for source in range(first, last)])


def tap_offsets(kernel_width):
    middle = kernel_width // 2
    result = []
    for along_x in range(kernel_width):
        for along_y in range(kernel_width):
            for along_z in range(kernel_width):
                result.append((along_x - middle, along_y - middle, along_z - middle))
    return result


def taps_stack(volume, kernel_width, direction):
    middle = kernel_width // 2
    padded = jnp.pad(volume, ((0, 0), (middle, middle), (middle, middle), (middle, middle)))
    size_x, size_y, size_z = (volume.shape[1], volume.shape[2], volume.shape[3])
    pieces = []
    for off_x, off_y, off_z in tap_offsets(kernel_width):
        start_x = middle + direction * off_x
        start_y = middle + direction * off_y
        start_z = middle + direction * off_z
        pieces.append(
            padded[
                :,
                start_x : start_x + size_x,
                start_y : start_y + size_y,
                start_z : start_z + size_z,
            ]
        )
    stacked = jnp.stack(pieces, 0)
    return stacked.reshape(len(pieces) * volume.shape[0], size_x * size_y * size_z)


def back_input(grad_out, w_rows):
    columns = taps_stack(grad_out, KW, -1)
    summed = lax.dot_general(
        w_rows, columns, (((0,), (0,)), ((), ())), preferred_element_type=jnp.float32
    )
    return summed.astype(jnp.bfloat16).reshape(grad_out.shape)


def back_weight(volume, grad_out):
    columns = taps_stack(volume, KW, 1)
    flattened = grad_out.reshape(grad_out.shape[0], -1)
    return lax.dot_general(
        columns, flattened, (((1,), (1,)), ((), ())), preferred_element_type=jnp.float32
    )


def local_inverse(matrix):
    values = matrix.astype(jnp.float32)
    step_size = 1.0 / jnp.max(jnp.sum(jnp.abs(values), axis=1))
    identity = jnp.eye(matrix.shape[0], dtype=jnp.float32)
    resid0 = (identity - step_size * values).astype(jnp.bfloat16)
    resid1 = jnp.dot(resid0, resid0, preferred_element_type=jnp.float32).astype(jnp.bfloat16)
    cross_term = jnp.dot(resid1, resid0, preferred_element_type=jnp.float32)
    return step_size * (
        identity + resid0.astype(jnp.float32) + resid1.astype(jnp.float32) + cross_term
    )


def eye_rows(start_row, row_total, order_full):
    column_ids = lax.broadcasted_iota(jnp.int32, (row_total, order_full), 1)
    row_ids = lax.broadcasted_iota(jnp.int32, (row_total, order_full), 0)
    return (column_ids == start_row + row_ids).astype(jnp.float32)


def halving_sum(value, axis, extra=None):
    count = lax.axis_size(axis)
    assert count & (count - 1) == 0 and value.shape[0] % count == 0
    index = lax.axis_index(axis)
    stride = 1
    while stride < count:
        half = value.shape[0] // 2
        upper = (index // stride) % 2 == 1
        keep = jnp.where(upper, value[half:], value[:half])
        send = jnp.where(upper, value[:half], value[half:])
        value = keep + lax.ppermute(send, axis, [(i, i ^ stride) for i in range(count)])
        stride *= 2
    if extra is not None:
        value = jnp.concatenate([value, extra], axis=0)
    stride = count // 2
    while stride >= 1:
        other = lax.ppermute(value, axis, [(i, i ^ stride) for i in range(count)])
        upper = (index // stride) % 2 == 1
        value = jnp.where(upper, jnp.concatenate([other, value]), jnp.concatenate([value, other]))
        stride //= 2
    if extra is None:
        return value
    pieces = value.reshape(count, -1, value.shape[1])
    held = pieces.shape[1] - extra.shape[0]
    return pieces[:, :held].reshape(-1, value.shape[1]), pieces[:, held:]


def compressed_products(gathered, a_rows, own_eye, shard_count, row_total, step_size):
    kept = shard_count // 2 + 1
    order_full = a_rows.shape[1]
    mirrored = shard_count - kept
    block_eye = jnp.logical_and(
        lax.broadcasted_iota(jnp.int32, gathered.shape, 1) == 0,
        lax.broadcasted_iota(jnp.int32, gathered.shape, 2)
        == lax.broadcasted_iota(jnp.int32, gathered.shape, 3),
    ).astype(jnp.float32)
    resid_blocks = (block_eye - step_size * gathered.astype(jnp.float32)).astype(jnp.bfloat16)
    doubled_right = jnp.concatenate([resid_blocks, resid_blocks], axis=0)
    direct_right = jnp.stack(
        [doubled_right[shard_count - offset : 2 * shard_count - offset, offset] for offset in range(kept)], 0
    )
    mirror_right = resid_blocks[:, 1 : mirrored + 1].transpose(1, 0, 2, 3)

    def times_resid0(left):
        doubled = jnp.concatenate([left, left], axis=0)
        direct_left = jnp.stack(
            [doubled[shard_count - offset : 2 * shard_count - offset] for offset in range(kept)], 0
        )
        mirror_left = jnp.stack(
            [doubled[offset : shard_count + offset] for offset in range(1, mirrored + 1)], 0
        )
        product = jnp.einsum(
            "kjab,kjbc->jac", direct_left, direct_right, preferred_element_type=jnp.float32
        ) + jnp.einsum(
            "mjab,mjcb->jac", mirror_left, mirror_right, preferred_element_type=jnp.float32
        )
        return product

    def as_rows(blocks):
        return blocks.transpose(1, 0, 2).reshape(row_total, order_full)

    resid0 = (own_eye - step_size * a_rows.astype(jnp.float32)).astype(jnp.bfloat16)
    resid1 = times_resid0(
        resid0.reshape(row_total, shard_count, row_total).transpose(1, 0, 2)
    ).astype(jnp.bfloat16)
    cross_term = times_resid0(resid1)
    return resid0, as_rows(resid1.astype(jnp.float32) + cross_term)


def dense_products(gathered, a_rows, own_eye):
    row_total = a_rows.shape[0]
    shard_count = gathered.shape[0]
    full_values = gathered.astype(jnp.float32)
    step_size = 1.0 / jnp.max(jnp.sum(jnp.abs(full_values), axis=2))
    block_ids = lax.broadcasted_iota(jnp.int32, gathered.shape, 0)
    row_ids = lax.broadcasted_iota(jnp.int32, gathered.shape, 1)
    column_ids = lax.broadcasted_iota(jnp.int32, gathered.shape, 2)
    full_eye = (column_ids == block_ids * row_total + row_ids).astype(jnp.float32)
    full_resid0 = (full_eye - step_size * full_values).astype(jnp.bfloat16)
    contract = (((1, 2), (0, 1)), ((), ()))
    resid0 = (own_eye - step_size * a_rows.astype(jnp.float32)).astype(jnp.bfloat16)
    resid1 = lax.dot_general(
        resid0.reshape(row_total, shard_count, row_total), full_resid0, contract,
        preferred_element_type=jnp.float32,
    ).astype(jnp.bfloat16)
    cross_term = lax.dot_general(
        resid1.reshape(row_total, shard_count, row_total), full_resid0, contract,
        preferred_element_type=jnp.float32,
    )
    return step_size, resid0, resid1, cross_term


def conv_back_input(grad_out, weights_now):
    channels = weights_now.shape[0]
    kernel = weights_now.reshape(channels, KW, KW, KW, channels)[:, ::-1, ::-1, ::-1, :]
    summed = lax.conv_general_dilated(
        grad_out[None], kernel.transpose(4, 0, 1, 2, 3), (1, 1, 1), ((KW // 2, KW // 2),) * 3,
        dimension_numbers=("NCDHW", "OIDHW", "NCDHW"), preferred_element_type=jnp.float32,
    )
    return summed[0].astype(jnp.bfloat16)


def conv_back_weight(volume, grad_out):
    channels = volume.shape[0]
    summed = lax.conv_general_dilated(
        volume[:, None], grad_out[:, None], (1, 1, 1), ((KW // 2, KW // 2),) * 3,
        dimension_numbers=("NCDHW", "OIDHW", "NCDHW"), preferred_element_type=jnp.float32,
    )
    return summed.transpose(2, 3, 4, 0, 1).reshape(KW ** 3 * channels, grad_out.shape[0])


def shards(acts, preacts, top_grad, weights, a_factor, g_factor):
    section_index = lax.axis_index("section")
    section_count = lax.axis_size("section")
    tick_count = MICRO + section_count - 1
    shard_count = lax.axis_size("dp")
    row_total = a_factor.shape[1]
    compressed = shard_count % 2 == 0 and row_total >= 64
    if compressed:
        kept = shard_count // 2 + 1
        own_blocks = a_factor[0].reshape(row_total, shard_count, row_total).transpose(1, 0, 2)
        twice = jnp.concatenate([own_blocks, own_blocks], axis=0)
        upper_blocks = lax.dynamic_slice_in_dim(twice, lax.axis_index("dp"), kept, 0)
        gathered = lax.all_gather(upper_blocks, "dp", axis=0)
    else:
        gathered = lax.all_gather(a_factor[0], "dp", axis=0)
    inputs = acts[0, 0]
    pre_values = preacts[0, 0]
    upper_grads = top_grad[0]
    micro_count = inputs.shape[0]
    zero_field = jnp.zeros(inputs.shape[1:], jnp.bfloat16)
    outgoing = zero_field
    stored_grads = [zero_field] * micro_count
    stored_slopes = [zero_field] * micro_count
    for tick_index in range(micro_count + section_count - 1):
        incoming = shifted(outgoing, "section", -1) if tick_index > 0 else zero_field
        micro_index = tick_index - (section_count - 1 - section_index)
        is_valid = jnp.logical_and(micro_index >= 0, micro_index < micro_count)
        clipped = jnp.clip(micro_index, 0, micro_count - 1)
        from_top = lax.dynamic_index_in_dim(upper_grads, clipped, 0, keepdims=False)
        arriving = jnp.where(section_index == section_count - 1, from_top, incoming)
        pre_now = lax.dynamic_index_in_dim(pre_values, clipped, 0, keepdims=False)
        grad_out = jnp.where(pre_now > 0, arriving, zero_field)
        outgoing = conv_back_input(grad_out, weights[0])
        for micro in range(micro_count):
            keep = jnp.logical_and(is_valid, clipped == micro)
            stored_grads[micro] = jnp.where(keep, outgoing, stored_grads[micro])
            stored_slopes[micro] = jnp.where(keep, grad_out, stored_slopes[micro])
    local_grad = conv_back_weight(inputs[0], stored_slopes[0])
    for micro in range(1, micro_count):
        local_grad = local_grad + conv_back_weight(inputs[micro], stored_slopes[micro])
    stored_grads = jnp.stack(stored_grads, 0)
    if compressed:
        local_largest = jnp.max(jnp.sum(jnp.abs(a_factor[0].astype(jnp.float32)), axis=1))
        carried = jnp.zeros((1, local_grad.shape[1]), jnp.float32).at[0, 0].set(local_largest)
        summed_grad, carried = halving_sum(local_grad, "dp", carried)
        step_size = 1.0 / jnp.max(carried[:, 0, 0])
    else:
        summed_grad = halving_sum(local_grad, "dp")
    mean_grad = summed_grad / lax.axis_size("dp")
    a_rows = a_factor[0]
    order_full = a_rows.shape[1]
    first_row = lax.axis_index("dp") * row_total
    own_eye = eye_rows(first_row, row_total, order_full)
    if compressed:
        resid0, later_terms = compressed_products(
            gathered, a_rows, own_eye, shard_count, row_total, step_size
        )
        inverse_rows = step_size * (own_eye + resid0.astype(jnp.float32) + later_terms)
    else:
        step_size, resid0, resid1, cross_term = dense_products(gathered, a_rows, own_eye)
        inverse_rows = step_size * (
            own_eye + resid0.astype(jnp.float32) + resid1.astype(jnp.float32) + cross_term
        )
    g_inverse = local_inverse(g_factor[0])
    preconditioned = jnp.dot(
        mean_grad, g_inverse, precision=lax.Precision.HIGHEST, preferred_element_type=jnp.float32
    )
    update_rows = jnp.dot(
        inverse_rows,
        preconditioned,
        precision=lax.Precision.HIGHEST,
        preferred_element_type=jnp.float32,
    )
    return (stored_grads[None, None], update_rows[None], inverse_rows[None])


def solution(mesh):
    placed = (
        P("section", "dp", None, None, None, None, None),
        P("section", "dp", None, None, None, None, None),
        P("dp", None, None, None, None, None),
        P("section", None, None),
        P("section", "dp", None),
        P("section", None, None),
    )
    return jax.shard_map(
        shards,
        mesh=mesh,
        in_specs=placed,
        out_specs=(
            P("section", "dp", None, None, None, None, None),
            P("section", "dp", None),
            P("section", "dp", None),
        ),
        check_vma=False,
    )
```

```python
import jax
import jax.numpy as jnp
from jax import lax
from jax.sharding import PartitionSpec as P

KW = 3
MICRO = 1


def shifted(value, axis, steps):
    count = lax.axis_size(axis)
    first, last = (max(0, -steps), min(count, count - steps))
    return lax.ppermute(value, axis, [(source, source + steps) for source in range(first, last)])


def tap_offsets(kernel_width):
    middle = kernel_width // 2
    result = []
    for along_x in range(kernel_width):
        for along_y in range(kernel_width):
            for along_z in range(kernel_width):
                result.append((along_x - middle, along_y - middle, along_z - middle))
    return result


def taps_stack(volume, kernel_width, direction):
    middle = kernel_width // 2
    padded = jnp.pad(volume, ((0, 0), (middle, middle), (middle, middle), (middle, middle)))
    size_x, size_y, size_z = (volume.shape[1], volume.shape[2], volume.shape[3])
    pieces = []
    for off_x, off_y, off_z in tap_offsets(kernel_width):
        start_x = middle + direction * off_x
        start_y = middle + direction * off_y
        start_z = middle + direction * off_z
        pieces.append(
            padded[
                :,
                start_x : start_x + size_x,
                start_y : start_y + size_y,
                start_z : start_z + size_z,
            ]
        )
    stacked = jnp.stack(pieces, 0)
    return stacked.reshape(len(pieces) * volume.shape[0], size_x * size_y * size_z)


def back_input(grad_out, w_rows):
    columns = taps_stack(grad_out, KW, -1)
    summed = lax.dot_general(
        w_rows, columns, (((0,), (0,)), ((), ())), preferred_element_type=jnp.float32
    )
    return summed.astype(jnp.bfloat16).reshape(grad_out.shape)


def back_weight(volume, grad_out):
    columns = taps_stack(volume, KW, 1)
    flattened = grad_out.reshape(grad_out.shape[0], -1)
    return lax.dot_general(
        columns, flattened, (((1,), (1,)), ((), ())), preferred_element_type=jnp.float32
    )


def local_inverse(matrix):
    values = matrix.astype(jnp.float32)
    step_size = 1.0 / jnp.max(jnp.sum(jnp.abs(values), axis=1))
    identity = jnp.eye(matrix.shape[0], dtype=jnp.float32)
    resid0 = (identity - step_size * values).astype(jnp.bfloat16)
    resid1 = jnp.dot(resid0, resid0, preferred_element_type=jnp.float32).astype(jnp.bfloat16)
    cross_term = jnp.dot(resid1, resid0, preferred_element_type=jnp.float32)
    return step_size * (
        identity + resid0.astype(jnp.float32) + resid1.astype(jnp.float32) + cross_term
    )


def eye_rows(start_row, row_total, order_full):
    column_ids = lax.broadcasted_iota(jnp.int32, (row_total, order_full), 1)
    row_ids = lax.broadcasted_iota(jnp.int32, (row_total, order_full), 0)
    return (column_ids == start_row + row_ids).astype(jnp.float32)


def halving_sum(value, axis, extra=None):
    count = lax.axis_size(axis)
    assert count & (count - 1) == 0 and value.shape[0] % count == 0
    index = lax.axis_index(axis)
    stride = 1
    while stride < count:
        half = value.shape[0] // 2
        upper = (index // stride) % 2 == 1
        keep = jnp.where(upper, value[half:], value[:half])
        send = jnp.where(upper, value[:half], value[half:])
        value = keep + lax.ppermute(send, axis, [(i, i ^ stride) for i in range(count)])
        stride *= 2
    if extra is not None:
        value = jnp.concatenate([value, extra], axis=0)
    stride = count // 2
    while stride >= 1:
        other = lax.ppermute(value, axis, [(i, i ^ stride) for i in range(count)])
        upper = (index // stride) % 2 == 1
        value = jnp.where(upper, jnp.concatenate([other, value]), jnp.concatenate([value, other]))
        stride //= 2
    if extra is None:
        return value
    pieces = value.reshape(count, -1, value.shape[1])
    held = pieces.shape[1] - extra.shape[0]
    return pieces[:, :held].reshape(-1, value.shape[1]), pieces[:, held:]


def compressed_products(gathered, a_rows, own_eye, shard_count, row_total, step_size):
    kept = shard_count // 2 + 1
    order_full = a_rows.shape[1]
    mirrored = shard_count - kept
    block_eye = jnp.logical_and(
        lax.broadcasted_iota(jnp.int32, gathered.shape, 1) == 0,
        lax.broadcasted_iota(jnp.int32, gathered.shape, 2)
        == lax.broadcasted_iota(jnp.int32, gathered.shape, 3),
    ).astype(jnp.float32)
    resid_blocks = (block_eye - step_size * gathered.astype(jnp.float32)).astype(jnp.bfloat16)
    doubled_right = jnp.concatenate([resid_blocks, resid_blocks], axis=0)
    direct_right = jnp.stack(
        [doubled_right[shard_count - offset : 2 * shard_count - offset, offset] for offset in range(kept)], 0
    )
    mirror_right = resid_blocks[:, 1 : mirrored + 1].transpose(1, 0, 2, 3)

    def times_resid0(left):
        doubled = jnp.concatenate([left, left], axis=0)
        direct_left = jnp.stack(
            [doubled[shard_count - offset : 2 * shard_count - offset] for offset in range(kept)], 0
        )
        mirror_left = jnp.stack(
            [doubled[offset : shard_count + offset] for offset in range(1, mirrored + 1)], 0
        )
        product = jnp.einsum(
            "kjab,kjbc->jac", direct_left, direct_right, preferred_element_type=jnp.float32
        ) + jnp.einsum(
            "mjab,mjcb->jac", mirror_left, mirror_right, preferred_element_type=jnp.float32
        )
        return product

    def as_rows(blocks):
        return blocks.transpose(1, 0, 2).reshape(row_total, order_full)

    resid0 = (own_eye - step_size * a_rows.astype(jnp.float32)).astype(jnp.bfloat16)
    resid1 = times_resid0(
        resid0.reshape(row_total, shard_count, row_total).transpose(1, 0, 2)
    ).astype(jnp.bfloat16)
    cross_term = times_resid0(resid1)
    return resid0, as_rows(resid1.astype(jnp.float32) + cross_term)


def dense_products(gathered, a_rows, own_eye):
    row_total = a_rows.shape[0]
    shard_count = gathered.shape[0]
    full_values = gathered.astype(jnp.float32)
    step_size = 1.0 / jnp.max(jnp.sum(jnp.abs(full_values), axis=2))
    block_ids = lax.broadcasted_iota(jnp.int32, gathered.shape, 0)
    row_ids = lax.broadcasted_iota(jnp.int32, gathered.shape, 1)
    column_ids = lax.broadcasted_iota(jnp.int32, gathered.shape, 2)
    full_eye = (column_ids == block_ids * row_total + row_ids).astype(jnp.float32)
    full_resid0 = (full_eye - step_size * full_values).astype(jnp.bfloat16)
    contract = (((1, 2), (0, 1)), ((), ()))
    resid0 = (own_eye - step_size * a_rows.astype(jnp.float32)).astype(jnp.bfloat16)
    resid1 = lax.dot_general(
        resid0.reshape(row_total, shard_count, row_total), full_resid0, contract,
        preferred_element_type=jnp.float32,
    ).astype(jnp.bfloat16)
    cross_term = lax.dot_general(
        resid1.reshape(row_total, shard_count, row_total), full_resid0, contract,
        preferred_element_type=jnp.float32,
    )
    return step_size, resid0, resid1, cross_term


def conv_back_input(grad_out, weights_now):
    channels = weights_now.shape[0]
    kernel = weights_now.reshape(channels, KW, KW, KW, channels)[:, ::-1, ::-1, ::-1, :]
    summed = lax.conv_general_dilated(
        grad_out[None], kernel.transpose(4, 0, 1, 2, 3), (1, 1, 1), ((KW // 2, KW // 2),) * 3,
        dimension_numbers=("NCDHW", "OIDHW", "NCDHW"), preferred_element_type=jnp.float32,
    )
    return summed[0].astype(jnp.bfloat16)


def conv_back_weight(volume, grad_out):
    channels = volume.shape[0]
    summed = lax.conv_general_dilated(
        volume[:, None], grad_out[:, None], (1, 1, 1), ((KW // 2, KW // 2),) * 3,
        dimension_numbers=("NCDHW", "OIDHW", "NCDHW"), preferred_element_type=jnp.float32,
    )
    return summed.transpose(2, 3, 4, 0, 1).reshape(KW ** 3 * channels, grad_out.shape[0])


def shards(acts, preacts, top_grad, weights, a_factor, g_factor):
    section_index = lax.axis_index("section")
    section_count = lax.axis_size("section")
    tick_count = MICRO + section_count - 1
    shard_count = lax.axis_size("dp")
    row_total = a_factor.shape[1]
    compressed = shard_count % 2 == 0 and row_total >= 64
    if compressed:
        kept = shard_count // 2 + 1
        upper_blocks = jnp.stack(
            [
                lax.dynamic_slice_in_dim(
                    a_factor[0], lax.rem(lax.axis_index("dp") + offset, shard_count) * row_total,
                    row_total, 1,
                )
                for offset in range(kept)
            ],
            0,
        )
        gathered = lax.all_gather(upper_blocks, "dp", axis=0)
    else:
        gathered = lax.all_gather(a_factor[0], "dp", axis=0)
    inputs = acts[0, 0]
    pre_values = preacts[0, 0]
    upper_grads = top_grad[0]
    micro_count = inputs.shape[0]
    zero_field = jnp.zeros(inputs.shape[1:], jnp.bfloat16)
    outgoing = zero_field
    stored_grads = [zero_field] * micro_count
    stored_slopes = [zero_field] * micro_count
    for tick_index in range(micro_count + section_count - 1):
        incoming = shifted(outgoing, "section", -1) if tick_index > 0 else zero_field
        micro_index = tick_index - (section_count - 1 - section_index)
        is_valid = jnp.logical_and(micro_index >= 0, micro_index < micro_count)
        clipped = jnp.clip(micro_index, 0, micro_count - 1)
        from_top = lax.dynamic_index_in_dim(upper_grads, clipped, 0, keepdims=False)
        arriving = jnp.where(section_index == section_count - 1, from_top, incoming)
        pre_now = lax.dynamic_index_in_dim(pre_values, clipped, 0, keepdims=False)
        grad_out = jnp.where(pre_now > 0, arriving, zero_field)
        outgoing = conv_back_input(grad_out, weights[0])
        for micro in range(micro_count):
            keep = jnp.logical_and(is_valid, clipped == micro)
            stored_grads[micro] = jnp.where(keep, outgoing, stored_grads[micro])
            stored_slopes[micro] = jnp.where(keep, grad_out, stored_slopes[micro])
    local_grad = conv_back_weight(inputs[0], stored_slopes[0])
    for micro in range(1, micro_count):
        local_grad = local_grad + conv_back_weight(inputs[micro], stored_slopes[micro])
    stored_grads = jnp.stack(stored_grads, 0)
    if compressed:
        local_largest = jnp.max(jnp.sum(jnp.abs(a_factor[0].astype(jnp.float32)), axis=1))
        carried = jnp.zeros((1, local_grad.shape[1]), jnp.float32).at[0, 0].set(local_largest)
        summed_grad, carried = halving_sum(local_grad, "dp", carried)
        step_size = 1.0 / jnp.max(carried[:, 0, 0])
    else:
        summed_grad = halving_sum(local_grad, "dp")
    mean_grad = summed_grad / lax.axis_size("dp")
    a_rows = a_factor[0]
    order_full = a_rows.shape[1]
    first_row = lax.axis_index("dp") * row_total
    own_eye = eye_rows(first_row, row_total, order_full)
    if compressed:
        resid0, later_terms = compressed_products(
            gathered, a_rows, own_eye, shard_count, row_total, step_size
        )
        inverse_rows = step_size * (own_eye + resid0.astype(jnp.float32) + later_terms)
    else:
        step_size, resid0, resid1, cross_term = dense_products(gathered, a_rows, own_eye)
        inverse_rows = step_size * (
            own_eye + resid0.astype(jnp.float32) + resid1.astype(jnp.float32) + cross_term
        )
    g_inverse = local_inverse(g_factor[0])
    preconditioned = jnp.dot(
        mean_grad, g_inverse, precision=lax.Precision.HIGH, preferred_element_type=jnp.float32
    )
    update_rows = jnp.dot(
        inverse_rows,
        preconditioned,
        precision=lax.Precision.HIGH,
        preferred_element_type=jnp.float32,
    )
    return (stored_grads[None, None], update_rows[None], inverse_rows[None])


def solution(mesh):
    placed = (
        P("section", "dp", None, None, None, None, None),
        P("section", "dp", None, None, None, None, None),
        P("dp", None, None, None, None, None),
        P("section", None, None),
        P("section", "dp", None),
        P("section", None, None),
    )
    return jax.shard_map(
        shards,
        mesh=mesh,
        in_specs=placed,
        out_specs=(
            P("section", "dp", None, None, None, None, None),
            P("section", "dp", None),
            P("section", "dp", None),
        ),
        check_vma=False,
    )
```

```python
import jax
import jax.numpy as jnp
from jax import lax
from jax.sharding import PartitionSpec as P

KW = 3
MICRO = 1


def shifted(value, axis, steps):
    count = lax.axis_size(axis)
    first, last = (max(0, -steps), min(count, count - steps))
    return lax.ppermute(value, axis, [(source, source + steps) for source in range(first, last)])


def tap_offsets(kernel_width):
    middle = kernel_width // 2
    result = []
    for along_x in range(kernel_width):
        for along_y in range(kernel_width):
            for along_z in range(kernel_width):
                result.append((along_x - middle, along_y - middle, along_z - middle))
    return result


def taps_stack(volume, kernel_width, direction):
    middle = kernel_width // 2
    padded = jnp.pad(volume, ((0, 0), (middle, middle), (middle, middle), (middle, middle)))
    size_x, size_y, size_z = (volume.shape[1], volume.shape[2], volume.shape[3])
    pieces = []
    for off_x, off_y, off_z in tap_offsets(kernel_width):
        start_x = middle + direction * off_x
        start_y = middle + direction * off_y
        start_z = middle + direction * off_z
        pieces.append(
            padded[
                :,
                start_x : start_x + size_x,
                start_y : start_y + size_y,
                start_z : start_z + size_z,
            ]
        )
    stacked = jnp.stack(pieces, 0)
    return stacked.reshape(len(pieces) * volume.shape[0], size_x * size_y * size_z)


def back_input(grad_out, w_rows):
    columns = taps_stack(grad_out, KW, -1)
    summed = lax.dot_general(
        w_rows, columns, (((0,), (0,)), ((), ())), preferred_element_type=jnp.float32
    )
    return summed.astype(jnp.bfloat16).reshape(grad_out.shape)


def back_weight(volume, grad_out):
    columns = taps_stack(volume, KW, 1)
    flattened = grad_out.reshape(grad_out.shape[0], -1)
    return lax.dot_general(
        columns, flattened, (((1,), (1,)), ((), ())), preferred_element_type=jnp.float32
    )


def local_inverse(matrix):
    values = matrix.astype(jnp.float32)
    step_size = 1.0 / jnp.max(jnp.sum(jnp.abs(values), axis=1))
    identity = jnp.eye(matrix.shape[0], dtype=jnp.float32)
    resid0 = (identity - step_size * values).astype(jnp.bfloat16)
    resid1 = jnp.dot(resid0, resid0, preferred_element_type=jnp.float32).astype(jnp.bfloat16)
    cross_term = jnp.dot(resid1, resid0, preferred_element_type=jnp.float32)
    return step_size * (
        identity + resid0.astype(jnp.float32) + resid1.astype(jnp.float32) + cross_term
    )


def eye_rows(start_row, row_total, order_full):
    column_ids = lax.broadcasted_iota(jnp.int32, (row_total, order_full), 1)
    row_ids = lax.broadcasted_iota(jnp.int32, (row_total, order_full), 0)
    return (column_ids == start_row + row_ids).astype(jnp.float32)


def halving_sum(value, axis, extra=None):
    count = lax.axis_size(axis)
    assert count & (count - 1) == 0 and value.shape[0] % count == 0
    index = lax.axis_index(axis)
    stride = 1
    while stride < count:
        half = value.shape[0] // 2
        upper = (index // stride) % 2 == 1
        keep = jnp.where(upper, value[half:], value[:half])
        send = jnp.where(upper, value[:half], value[half:])
        value = keep + lax.ppermute(send, axis, [(i, i ^ stride) for i in range(count)])
        stride *= 2
    if extra is not None:
        value = jnp.concatenate([value, extra], axis=0)
    stride = count // 2
    while stride >= 1:
        other = lax.ppermute(value, axis, [(i, i ^ stride) for i in range(count)])
        upper = (index // stride) % 2 == 1
        value = jnp.where(upper, jnp.concatenate([other, value]), jnp.concatenate([value, other]))
        stride //= 2
    if extra is None:
        return value
    pieces = value.reshape(count, -1, value.shape[1])
    held = pieces.shape[1] - extra.shape[0]
    return pieces[:, :held].reshape(-1, value.shape[1]), pieces[:, held:]


def compressed_products(gathered, a_rows, own_eye, shard_count, row_total, step_size):
    kept = shard_count // 2 + 1
    order_full = a_rows.shape[1]
    mirrored = shard_count - kept
    block_eye = jnp.logical_and(
        lax.broadcasted_iota(jnp.int32, gathered.shape, 1) == 0,
        lax.broadcasted_iota(jnp.int32, gathered.shape, 2)
        == lax.broadcasted_iota(jnp.int32, gathered.shape, 3),
    ).astype(jnp.float32)
    resid_blocks = (block_eye - step_size * gathered.astype(jnp.float32)).astype(jnp.bfloat16)
    doubled_right = jnp.concatenate([resid_blocks, resid_blocks], axis=0)
    direct_right = jnp.stack(
        [doubled_right[shard_count - offset : 2 * shard_count - offset, offset] for offset in range(kept)], 0
    )
    mirror_right = resid_blocks[:, 1 : mirrored + 1].transpose(1, 0, 2, 3)

    def times_resid0(left):
        doubled = jnp.concatenate([left, left], axis=0)
        direct_left = jnp.stack(
            [doubled[shard_count - offset : 2 * shard_count - offset] for offset in range(kept)], 0
        )
        mirror_left = jnp.stack(
            [doubled[offset : shard_count + offset] for offset in range(1, mirrored + 1)], 0
        )
        product = jnp.einsum(
            "kjab,kjbc->jac", direct_left, direct_right, preferred_element_type=jnp.float32
        ) + jnp.einsum(
            "mjab,mjcb->jac", mirror_left, mirror_right, preferred_element_type=jnp.float32
        )
        return product

    def as_rows(blocks):
        return blocks.transpose(1, 0, 2).reshape(row_total, order_full)

    resid0 = (own_eye - step_size * a_rows.astype(jnp.float32)).astype(jnp.bfloat16)
    resid1 = times_resid0(
        resid0.reshape(row_total, shard_count, row_total).transpose(1, 0, 2)
    ).astype(jnp.bfloat16)
    cross_term = times_resid0(resid1)
    return resid0, as_rows(resid1.astype(jnp.float32) + cross_term)


def dense_products(gathered, a_rows, own_eye):
    row_total = a_rows.shape[0]
    shard_count = gathered.shape[0]
    full_values = gathered.astype(jnp.float32)
    step_size = 1.0 / jnp.max(jnp.sum(jnp.abs(full_values), axis=2))
    block_ids = lax.broadcasted_iota(jnp.int32, gathered.shape, 0)
    row_ids = lax.broadcasted_iota(jnp.int32, gathered.shape, 1)
    column_ids = lax.broadcasted_iota(jnp.int32, gathered.shape, 2)
    full_eye = (column_ids == block_ids * row_total + row_ids).astype(jnp.float32)
    full_resid0 = (full_eye - step_size * full_values).astype(jnp.bfloat16)
    contract = (((1, 2), (0, 1)), ((), ()))
    resid0 = (own_eye - step_size * a_rows.astype(jnp.float32)).astype(jnp.bfloat16)
    resid1 = lax.dot_general(
        resid0.reshape(row_total, shard_count, row_total), full_resid0, contract,
        preferred_element_type=jnp.float32,
    ).astype(jnp.bfloat16)
    cross_term = lax.dot_general(
        resid1.reshape(row_total, shard_count, row_total), full_resid0, contract,
        preferred_element_type=jnp.float32,
    )
    return step_size, resid0, resid1, cross_term


def conv_back_input(grad_out, weights_now):
    channels = weights_now.shape[0]
    kernel = weights_now.reshape(channels, KW, KW, KW, channels)[:, ::-1, ::-1, ::-1, :]
    summed = lax.conv_general_dilated(
        grad_out[None], kernel.transpose(4, 0, 1, 2, 3), (1, 1, 1), ((KW // 2, KW // 2),) * 3,
        dimension_numbers=("NCDHW", "OIDHW", "NCDHW"), preferred_element_type=jnp.float32,
    )
    return summed[0].astype(jnp.bfloat16)


def conv_back_weight(volume, grad_out):
    channels = volume.shape[0]
    summed = lax.conv_general_dilated(
        volume[:, None], grad_out[:, None], (1, 1, 1), ((KW // 2, KW // 2),) * 3,
        dimension_numbers=("NCDHW", "OIDHW", "NCDHW"), preferred_element_type=jnp.float32,
    )
    return summed.transpose(2, 3, 4, 0, 1).reshape(KW ** 3 * channels, grad_out.shape[0])


def shards(acts, preacts, top_grad, weights, a_factor, g_factor):
    section_index = lax.axis_index("section")
    section_count = lax.axis_size("section")
    tick_count = MICRO + section_count - 1
    shard_count = lax.axis_size("dp")
    row_total = a_factor.shape[1]
    compressed = shard_count % 2 == 0 and row_total >= 64
    if compressed:
        kept = shard_count // 2 + 1
        own_blocks = a_factor[0].reshape(row_total, shard_count, row_total).transpose(1, 0, 2)
        twice = jnp.concatenate([own_blocks, own_blocks], axis=0)
        upper_blocks = lax.dynamic_slice_in_dim(twice, lax.axis_index("dp"), kept, 0)
        gathered = lax.all_gather(upper_blocks, "dp", axis=0)
    else:
        gathered = lax.all_gather(a_factor[0], "dp", axis=0)
    inputs = acts[0, 0]
    pre_values = preacts[0, 0]
    upper_grads = top_grad[0]
    micro_count = inputs.shape[0]
    zero_field = jnp.zeros(inputs.shape[1:], jnp.bfloat16)
    outgoing = zero_field
    stored_grads = [zero_field] * micro_count
    stored_slopes = [zero_field] * micro_count
    for tick_index in range(micro_count + section_count - 1):
        incoming = shifted(outgoing, "section", -1) if tick_index > 0 else zero_field
        micro_index = tick_index - (section_count - 1 - section_index)
        is_valid = jnp.logical_and(micro_index >= 0, micro_index < micro_count)
        clipped = jnp.clip(micro_index, 0, micro_count - 1)
        from_top = lax.dynamic_index_in_dim(upper_grads, clipped, 0, keepdims=False)
        arriving = jnp.where(section_index == section_count - 1, from_top, incoming)
        pre_now = lax.dynamic_index_in_dim(pre_values, clipped, 0, keepdims=False)
        grad_out = jnp.where(pre_now > 0, arriving, zero_field)
        outgoing = conv_back_input(grad_out, weights[0])
        for micro in range(micro_count):
            keep = jnp.logical_and(is_valid, clipped == micro)
            stored_grads[micro] = jnp.where(keep, outgoing, stored_grads[micro])
            stored_slopes[micro] = jnp.where(keep, grad_out, stored_slopes[micro])
    local_grad = conv_back_weight(inputs[0], stored_slopes[0])
    for micro in range(1, micro_count):
        local_grad = local_grad + conv_back_weight(inputs[micro], stored_slopes[micro])
    stored_grads = jnp.stack(stored_grads, 0)
    if compressed:
        local_largest = jnp.max(jnp.sum(jnp.abs(a_factor[0].astype(jnp.float32)), axis=1))
        carried = jnp.zeros((1, local_grad.shape[1]), jnp.float32).at[0, 0].set(local_largest)
        summed_grad, carried = halving_sum(local_grad, "dp", carried)
        step_size = 1.0 / jnp.max(carried[:, 0, 0])
    else:
        summed_grad = halving_sum(local_grad, "dp")
    mean_grad = summed_grad / lax.axis_size("dp")
    a_rows = a_factor[0]
    order_full = a_rows.shape[1]
    first_row = lax.axis_index("dp") * row_total
    own_eye = eye_rows(first_row, row_total, order_full)
    if compressed:
        resid0, later_terms = compressed_products(
            gathered, a_rows, own_eye, shard_count, row_total, step_size
        )
        inverse_rows = step_size * (own_eye + resid0.astype(jnp.float32) + later_terms)
    else:
        step_size, resid0, resid1, cross_term = dense_products(gathered, a_rows, own_eye)
        inverse_rows = step_size * (
            own_eye + resid0.astype(jnp.float32) + resid1.astype(jnp.float32) + cross_term
        )
    g_inverse = local_inverse(g_factor[0])
    preconditioned = jnp.dot(
        mean_grad, g_inverse, precision=lax.Precision.HIGH, preferred_element_type=jnp.float32
    )
    update_rows = jnp.dot(
        inverse_rows,
        preconditioned,
        precision=lax.Precision.HIGH,
        preferred_element_type=jnp.float32,
    )
    return (stored_grads[None, None], update_rows[None], inverse_rows[None])


def solution(mesh):
    placed = (
        P("section", "dp", None, None, None, None, None),
        P("section", "dp", None, None, None, None, None),
        P("dp", None, None, None, None, None),
        P("section", None, None),
        P("section", "dp", None),
        P("section", None, None),
    )
    return jax.shard_map(
        shards,
        mesh=mesh,
        in_specs=placed,
        out_specs=(
            P("section", "dp", None, None, None, None, None),
            P("section", "dp", None),
            P("section", "dp", None),
        ),
        check_vma=False,
    )
```

```python
import jax
import jax.numpy as jnp
from jax import lax
from jax.sharding import PartitionSpec as P

KW = 3
MICRO = 1


def shifted(value, axis, steps):
    count = lax.axis_size(axis)
    first, last = (max(0, -steps), min(count, count - steps))
    return lax.ppermute(value, axis, [(source, source + steps) for source in range(first, last)])


def tap_offsets(kernel_width):
    middle = kernel_width // 2
    result = []
    for along_x in range(kernel_width):
        for along_y in range(kernel_width):
            for along_z in range(kernel_width):
                result.append((along_x - middle, along_y - middle, along_z - middle))
    return result


def taps_stack(volume, kernel_width, direction):
    middle = kernel_width // 2
    padded = jnp.pad(volume, ((0, 0), (middle, middle), (middle, middle), (middle, middle)))
    size_x, size_y, size_z = (volume.shape[1], volume.shape[2], volume.shape[3])
    pieces = []
    for off_x, off_y, off_z in tap_offsets(kernel_width):
        start_x = middle + direction * off_x
        start_y = middle + direction * off_y
        start_z = middle + direction * off_z
        pieces.append(
            padded[
                :,
                start_x : start_x + size_x,
                start_y : start_y + size_y,
                start_z : start_z + size_z,
            ]
        )
    stacked = jnp.stack(pieces, 0)
    return stacked.reshape(len(pieces) * volume.shape[0], size_x * size_y * size_z)


def back_input(grad_out, w_rows):
    columns = taps_stack(grad_out, KW, -1)
    summed = lax.dot_general(
        w_rows, columns, (((0,), (0,)), ((), ())), preferred_element_type=jnp.float32
    )
    return summed.astype(jnp.bfloat16).reshape(grad_out.shape)


def back_weight(volume, grad_out):
    columns = taps_stack(volume, KW, 1)
    flattened = grad_out.reshape(grad_out.shape[0], -1)
    return lax.dot_general(
        columns, flattened, (((1,), (1,)), ((), ())), preferred_element_type=jnp.float32
    )


def local_inverse(matrix):
    values = matrix.astype(jnp.float32)
    step_size = 1.0 / jnp.max(jnp.sum(jnp.abs(values), axis=1))
    identity = jnp.eye(matrix.shape[0], dtype=jnp.float32)
    resid0 = (identity - step_size * values).astype(jnp.bfloat16)
    resid1 = jnp.dot(resid0, resid0, preferred_element_type=jnp.float32).astype(jnp.bfloat16)
    cross_term = jnp.dot(resid1, resid0, preferred_element_type=jnp.float32)
    return step_size * (
        identity + resid0.astype(jnp.float32) + resid1.astype(jnp.float32) + cross_term
    )


def eye_rows(start_row, row_total, order_full):
    column_ids = lax.broadcasted_iota(jnp.int32, (row_total, order_full), 1)
    row_ids = lax.broadcasted_iota(jnp.int32, (row_total, order_full), 0)
    return (column_ids == start_row + row_ids).astype(jnp.float32)


def halving_sum(value, axis, extra=None):
    count = lax.axis_size(axis)
    assert count & (count - 1) == 0 and value.shape[0] % count == 0
    index = lax.axis_index(axis)
    stride = 1
    while stride < count:
        half = value.shape[0] // 2
        upper = (index // stride) % 2 == 1
        keep = jnp.where(upper, value[half:], value[:half])
        send = jnp.where(upper, value[:half], value[half:])
        value = keep + lax.ppermute(send, axis, [(i, i ^ stride) for i in range(count)])
        stride *= 2
    if extra is not None:
        value = jnp.concatenate([value, extra], axis=0)
    stride = count // 2
    while stride >= 1:
        other = lax.ppermute(value, axis, [(i, i ^ stride) for i in range(count)])
        upper = (index // stride) % 2 == 1
        value = jnp.where(upper, jnp.concatenate([other, value]), jnp.concatenate([value, other]))
        stride //= 2
    if extra is None:
        return value
    pieces = value.reshape(count, -1, value.shape[1])
    held = pieces.shape[1] - extra.shape[0]
    return pieces[:, :held].reshape(-1, value.shape[1]), pieces[:, held:]


def compressed_products(gathered, a_rows, own_eye, shard_count, row_total, step_size):
    kept = shard_count // 2 + 1
    order_full = a_rows.shape[1]
    mirrored = shard_count - kept
    block_eye = jnp.logical_and(
        lax.broadcasted_iota(jnp.int32, gathered.shape, 1) == 0,
        lax.broadcasted_iota(jnp.int32, gathered.shape, 2)
        == lax.broadcasted_iota(jnp.int32, gathered.shape, 3),
    ).astype(jnp.float32)
    resid_blocks = (block_eye - step_size * gathered.astype(jnp.float32)).astype(jnp.bfloat16)
    doubled_right = jnp.concatenate([resid_blocks, resid_blocks], axis=0)
    direct_right = jnp.stack(
        [doubled_right[shard_count - offset : 2 * shard_count - offset, offset] for offset in range(kept)], 0
    )
    mirror_right = resid_blocks[:, 1 : mirrored + 1].transpose(1, 0, 2, 3)

    def times_resid0(left):
        doubled = jnp.concatenate([left, left], axis=0)
        direct_left = jnp.stack(
            [doubled[shard_count - offset : 2 * shard_count - offset] for offset in range(kept)], 0
        )
        mirror_left = jnp.stack(
            [doubled[offset : shard_count + offset] for offset in range(1, mirrored + 1)], 0
        )
        product = jnp.einsum(
            "kjab,kjbc->jac", direct_left, direct_right, preferred_element_type=jnp.float32
        ) + jnp.einsum(
            "mjab,mjcb->jac", mirror_left, mirror_right, preferred_element_type=jnp.float32
        )
        return product

    def as_rows(blocks):
        return blocks.transpose(1, 0, 2).reshape(row_total, order_full)

    resid0 = (own_eye - step_size * a_rows.astype(jnp.float32)).astype(jnp.bfloat16)
    resid1 = times_resid0(
        resid0.reshape(row_total, shard_count, row_total).transpose(1, 0, 2)
    ).astype(jnp.bfloat16)
    cross_term = times_resid0(resid1)
    return resid0, as_rows(resid1.astype(jnp.float32) + cross_term)


def dense_products(gathered, a_rows, own_eye):
    row_total = a_rows.shape[0]
    shard_count = gathered.shape[0]
    full_values = gathered.astype(jnp.float32)
    step_size = 1.0 / jnp.max(jnp.sum(jnp.abs(full_values), axis=2))
    block_ids = lax.broadcasted_iota(jnp.int32, gathered.shape, 0)
    row_ids = lax.broadcasted_iota(jnp.int32, gathered.shape, 1)
    column_ids = lax.broadcasted_iota(jnp.int32, gathered.shape, 2)
    full_eye = (column_ids == block_ids * row_total + row_ids).astype(jnp.float32)
    full_resid0 = (full_eye - step_size * full_values).astype(jnp.bfloat16)
    contract = (((1, 2), (0, 1)), ((), ()))
    resid0 = (own_eye - step_size * a_rows.astype(jnp.float32)).astype(jnp.bfloat16)
    resid1 = lax.dot_general(
        resid0.reshape(row_total, shard_count, row_total), full_resid0, contract,
        preferred_element_type=jnp.float32,
    ).astype(jnp.bfloat16)
    cross_term = lax.dot_general(
        resid1.reshape(row_total, shard_count, row_total), full_resid0, contract,
        preferred_element_type=jnp.float32,
    )
    return step_size, resid0, resid1, cross_term


def conv_back_input(grad_out, weights_now):
    channels = weights_now.shape[0]
    kernel = weights_now.reshape(channels, KW, KW, KW, channels)[:, ::-1, ::-1, ::-1, :]
    summed = lax.conv_general_dilated(
        grad_out[None], kernel.transpose(4, 0, 1, 2, 3), (1, 1, 1), ((KW // 2, KW // 2),) * 3,
        dimension_numbers=("NCDHW", "OIDHW", "NCDHW"), preferred_element_type=jnp.float32,
    )
    return summed[0].astype(jnp.bfloat16)


def conv_back_weight(volume, grad_out):
    channels = volume.shape[0]
    summed = lax.conv_general_dilated(
        volume[:, None], grad_out[:, None], (1, 1, 1), ((KW // 2, KW // 2),) * 3,
        dimension_numbers=("NCDHW", "OIDHW", "NCDHW"), preferred_element_type=jnp.float32,
    )
    return summed.transpose(2, 3, 4, 0, 1).reshape(KW ** 3 * channels, grad_out.shape[0])


def shards(acts, preacts, top_grad, weights, a_factor, g_factor):
    section_index = lax.axis_index("section")
    section_count = lax.axis_size("section")
    tick_count = MICRO + section_count - 1
    shard_count = lax.axis_size("dp")
    row_total = a_factor.shape[1]
    compressed = shard_count % 2 == 0 and row_total >= 64
    if compressed:
        kept = shard_count // 2 + 1
        own_blocks = a_factor[0].reshape(row_total, shard_count, row_total).transpose(1, 0, 2)
        twice = jnp.concatenate([own_blocks, own_blocks], axis=0)
        upper_blocks = lax.dynamic_slice_in_dim(twice, lax.axis_index("dp"), kept, 0)
        gathered = lax.all_gather(upper_blocks.reshape(-1), "dp", axis=0).reshape(
            (shard_count,) + upper_blocks.shape
        )
    else:
        gathered = lax.all_gather(a_factor[0], "dp", axis=0)
    inputs = acts[0, 0]
    pre_values = preacts[0, 0]
    upper_grads = top_grad[0]
    micro_count = inputs.shape[0]
    zero_field = jnp.zeros(inputs.shape[1:], jnp.bfloat16)
    outgoing = zero_field
    stored_grads = [zero_field] * micro_count
    stored_slopes = [zero_field] * micro_count
    for tick_index in range(micro_count + section_count - 1):
        incoming = shifted(outgoing, "section", -1) if tick_index > 0 else zero_field
        micro_index = tick_index - (section_count - 1 - section_index)
        is_valid = jnp.logical_and(micro_index >= 0, micro_index < micro_count)
        clipped = jnp.clip(micro_index, 0, micro_count - 1)
        from_top = lax.dynamic_index_in_dim(upper_grads, clipped, 0, keepdims=False)
        arriving = jnp.where(section_index == section_count - 1, from_top, incoming)
        pre_now = lax.dynamic_index_in_dim(pre_values, clipped, 0, keepdims=False)
        grad_out = jnp.where(pre_now > 0, arriving, zero_field)
        outgoing = conv_back_input(grad_out, weights[0])
        for micro in range(micro_count):
            keep = jnp.logical_and(is_valid, clipped == micro)
            stored_grads[micro] = jnp.where(keep, outgoing, stored_grads[micro])
            stored_slopes[micro] = jnp.where(keep, grad_out, stored_slopes[micro])
    local_grad = conv_back_weight(inputs[0], stored_slopes[0])
    for micro in range(1, micro_count):
        local_grad = local_grad + conv_back_weight(inputs[micro], stored_slopes[micro])
    stored_grads = jnp.stack(stored_grads, 0)
    if compressed:
        local_largest = jnp.max(jnp.sum(jnp.abs(a_factor[0].astype(jnp.float32)), axis=1))
        carried = jnp.zeros((1, local_grad.shape[1]), jnp.float32).at[0, 0].set(local_largest)
        summed_grad, carried = halving_sum(local_grad, "dp", carried)
        step_size = 1.0 / jnp.max(carried[:, 0, 0])
    else:
        summed_grad = halving_sum(local_grad, "dp")
    mean_grad = summed_grad / lax.axis_size("dp")
    a_rows = a_factor[0]
    order_full = a_rows.shape[1]
    first_row = lax.axis_index("dp") * row_total
    own_eye = eye_rows(first_row, row_total, order_full)
    if compressed:
        resid0, later_terms = compressed_products(
            gathered, a_rows, own_eye, shard_count, row_total, step_size
        )
        inverse_rows = step_size * (own_eye + resid0.astype(jnp.float32) + later_terms)
    else:
        step_size, resid0, resid1, cross_term = dense_products(gathered, a_rows, own_eye)
        inverse_rows = step_size * (
            own_eye + resid0.astype(jnp.float32) + resid1.astype(jnp.float32) + cross_term
        )
    g_inverse = local_inverse(g_factor[0])
    preconditioned = jnp.dot(
        mean_grad, g_inverse, precision=lax.Precision.HIGHEST, preferred_element_type=jnp.float32
    )
    update_rows = jnp.dot(
        inverse_rows,
        preconditioned,
        precision=lax.Precision.HIGHEST,
        preferred_element_type=jnp.float32,
    )
    return (stored_grads[None, None], update_rows[None], inverse_rows[None])


def solution(mesh):
    placed = (
        P("section", "dp", None, None, None, None, None),
        P("section", "dp", None, None, None, None, None),
        P("dp", None, None, None, None, None),
        P("section", None, None),
        P("section", "dp", None),
        P("section", None, None),
    )
    return jax.shard_map(
        shards,
        mesh=mesh,
        in_specs=placed,
        out_specs=(
            P("section", "dp", None, None, None, None, None),
            P("section", "dp", None),
            P("section", "dp", None),
        ),
        check_vma=False,
    )
```
